32 devices in a mesh: clips: 2 (over x), rows: 16 (over z, y, core).
Axes of the slice: x: 2, y: 2, z: 4, core: 2. Of those that a mesh axis runs over, the one named last changes fastest.
Arguments:
- frames: bfloat16 [2, 32, 128, 384], P('clips', 'rows'), parts along dimension 0, may hold values from -48 to 48
- norm_attn: float32 [384], replicated, may hold values from 0.25 to 1.75
- w_query: bfloat16 [384, 384], replicated, may hold values from -12 to 12
- w_key: bfloat16 [384, 384], replicated, may hold values from -12 to 12
- w_value: bfloat16 [384, 384], replicated, may hold values from -2 to 2
- w_out: bfloat16 [384, 384], replicated, may hold values from -9 to 9
- cache_one: bfloat16 [4, 32, 128, 384], P('clips', 'rows'), parts along dimension 0, may hold values from -6 to 6
- norm_conv: float32 [384], replicated, may hold values from 0.25 to 1.75
- conv_weight: bfloat16 [3, 3, 3, 384, 384], replicated, may hold values from -0.109375 to 0.109375
- w_up: bfloat16 [3, 3, 384, 192], replicated, may hold values from -0.109375 to 0.109375
Outputs:
- upsampled: bfloat16 [2, 64, 49152], P('clips', 'rows'), parts along dimension 0
The draws below stay inside these ranges and needn't reach their ends.
There are 2 independent parts, one for each index of `clips`. The reference program is written for one: setup_inputs(seed, part) draws one part's arguments, and reference() takes and returns one part's arrays. A program takes and returns all parts, laid end to end along the dimension named above; an argument that names none is the same for every part. Nothing has to cross between parts.
All inputs are finite; a program needn't handle non-finite values.
Results may differ from the reference program's by a relative error of at most 0.013.
Values may be sent and summed in bfloat16 or wider, within the bound.
No kernel may reach another device: no remote copies, remote signals or barrier semaphores. Data moves between devices by JAX's collectives and lax.ppermute only.
A program may use at most 128 MiB of HBM per device.

```python
import math
import jax
import jax.numpy as jnp
from jax import lax

C = 384
OUTC = 192
W = 128
FR = 1
H = 32


def near_permute(key):
    order = jax.random.permutation(jax.random.fold_in(key, 1), C)
    onehot = (jnp.arange(C)[None, :] == order[:, None]).astype(jnp.float32)
    signs = (2 * jax.random.randint(jax.random.fold_in(key, 2), (C, 1), 0, 2) - 1).astype(jnp.float32)
    noise = jnp.clip(jax.random.normal(jax.random.fold_in(key, 3), (C, C), jnp.float32), -4.0, 4.0) / math.sqrt(C)
    return 0.9 * signs * onehot + 0.3 * noise


def attn_pair(key):
    base = jax.random.fold_in(key, 11)
    first = near_permute(jax.random.fold_in(base, 1))
    second = near_permute(jax.random.fold_in(base, 2))
    return (first * 1.6, second * 1.6)


def draw_w_query(key, part):
    return attn_pair(key)[0].astype(jnp.bfloat16)


def draw_w_key(key, part):
    return attn_pair(key)[1].astype(jnp.bfloat16)


def draw_w_value(key, part):
    base = jax.random.fold_in(key, 31)
    result = near_permute(jax.random.fold_in(base, 1))
    return result.astype(jnp.bfloat16)


def draw_w_out(key, part):
    base = jax.random.fold_in(key, 41)
    result = near_permute(jax.random.fold_in(base, 1)) * 5.0
    return result.astype(jnp.bfloat16)


def draw_frames(key, part):
    first = jax.random.fold_in(key, 21)
    result = jnp.clip(jax.random.normal(jax.random.fold_in(first, 1), (FR, H, W, C), jnp.float32), -6.0, 6.0)
    return result.astype(jnp.bfloat16)


def block_scale(own_key, extent, shards, least, high):
    def one(dim, parts):
        steps = jax.random.uniform(jax.random.fold_in(jax.random.fold_in(own_key, 6), dim), (parts,), jnp.float32, least / len(shards), high / len(shards))
        return jnp.repeat(jnp.exp(steps), extent[dim] // parts).reshape((-1,) + (1,) * (len(extent) - dim - 1))

    loudness = one(*shards[0])
    for cut in shards[1:]:
        loudness = loudness * one(*cut)
    return loudness


def centred(own_key, shape, width, bound, cuts=(), held_as=jnp.bfloat16):
    factor_of = block_scale(own_key, shape, cuts, -0.22, 0.18) if cuts else 1.0
    array = jax.random.normal(own_key, shape, jnp.float32) * width * factor_of
    return jnp.minimum(jnp.maximum(array, -bound), bound).astype(held_as)


def setup_inputs(seed: int = 0, part: int = 0) -> dict:
    key_of = jax.random.split(jax.random.key(seed), 11)
    own_keys = jax.random.split(jax.random.fold_in(key_of[10], part), 11)
    return {
        "frames": draw_frames(jax.random.fold_in(jax.random.fold_in(key_of[10], part), 71), part),
        "norm_attn": jnp.clip(1.0 + 0.15 * jax.random.normal(key_of[1], (C,), jnp.float32), 0.25, 1.75),
        "w_query": draw_w_query(jax.random.fold_in(key_of[10], 71), part),
        "w_key": draw_w_key(jax.random.fold_in(key_of[10], 71), part),
        "w_value": draw_w_value(jax.random.fold_in(key_of[10], 71), part),
        "w_out": draw_w_out(jax.random.fold_in(key_of[10], 71), part),
        "cache_one": centred(own_keys[6], (2, H, W, C), 1.0, 6.0, ((1, 16),)),
        "norm_conv": jnp.clip(1.0 + 0.15 * jax.random.normal(key_of[7], (C,), jnp.float32), 0.25, 1.75),
        "conv_weight": centred(key_of[8], (3, 3, 3, C, C), (9 * C) ** -0.5, 0.109375),
        "w_up": centred(key_of[9], (3, 3, C, OUTC), (9 * C) ** -0.5, 0.109375),
    }


EPS = 1e-06

def rms_gain(values, gain):
    return values * lax.rsqrt(lax.optimization_barrier(jnp.mean(values * values, axis=-1, keepdims=True)) + EPS) * gain.astype(jnp.float32)

def conv_core(padded, weight, frames_out, rows_out, cols_out):
    chans = padded.shape[-1]
    outs = weight.shape[-1]
    wide = jnp.concatenate([padded[:, :, shift:shift + cols_out, :] for shift in range(3)], axis=-1)
    total = jnp.zeros((frames_out * rows_out * cols_out, outs), jnp.float32)
    for tstep in range(weight.shape[0]):
        for rstep in range(3):
            part = wide[tstep:tstep + frames_out, rstep:rstep + rows_out].reshape(-1, 3 * chans)
            total = total + jnp.dot(part, weight[tstep, rstep].reshape(3 * chans, outs), preferred_element_type=jnp.float32)
    return total

def reference(frames, norm_attn, w_query, w_key, w_value, w_out, cache_one, norm_conv, conv_weight, w_up):
    count = H * W
    flat = frames.reshape(FR * count, C)
    normed = rms_gain(flat.astype(jnp.float32), norm_attn).astype(jnp.bfloat16)
    queries = jnp.dot(normed, w_query, preferred_element_type=jnp.float32).astype(jnp.bfloat16).reshape(FR, count, C)
    keys = jnp.dot(normed, w_key, preferred_element_type=jnp.float32).astype(jnp.bfloat16).reshape(FR, count, C)
    values = jnp.dot(normed, w_value, preferred_element_type=jnp.float32).astype(jnp.bfloat16).reshape(FR, count, C)
    block = math.gcd(1024, count)
    scale = C ** (-0.5)

    def attend_frame(triple):
        frame_q, frame_k, frame_v = triple

        def one_block(rows_q):
            scores = jnp.dot(rows_q, frame_k.T, preferred_element_type=jnp.float32) * scale
            top = lax.optimization_barrier(jnp.max(scores, axis=-1, keepdims=True))
            expo = jnp.exp(scores - top)
            numer = jnp.dot(expo.astype(jnp.bfloat16), frame_v, preferred_element_type=jnp.float32)
            return (numer / lax.optimization_barrier(jnp.sum(expo, axis=-1, keepdims=True))).astype(jnp.bfloat16)
        return lax.map(one_block, frame_q.reshape(count // block, block, C)).reshape(count, C)
    attended = lax.map(attend_frame, (queries, keys, values)).reshape(FR * count, C)
    mixed = (flat.astype(jnp.float32) + jnp.dot(attended, w_out, preferred_element_type=jnp.float32)).astype(jnp.bfloat16)
    activ = jax.nn.silu(rms_gain(mixed.astype(jnp.float32), norm_conv)).astype(jnp.bfloat16).reshape(FR, H, W, C)
    stack = jnp.concatenate([cache_one, activ], axis=0)
    padded = jnp.pad(stack, ((0, 0), (1, 1), (1, 1), (0, 0)))
    conv_out = conv_core(padded, conv_weight, FR, H, W).astype(jnp.bfloat16).reshape(FR, H, W, C)
    doubled = jnp.repeat(jnp.repeat(conv_out, 2, axis=1), 2, axis=2)
    padded_up = jnp.pad(doubled, ((0, 0), (1, 1), (1, 1), (0, 0)))
    result = conv_core(padded_up, w_up[None], FR, 2 * H, 2 * W)
    return result.astype(jnp.bfloat16).reshape(FR, 2 * H, 2 * W * OUTC)
```

```python
import jax
import jax.numpy as jnp
from jax import lax
from jax.sharding import PartitionSpec as P

EPS = 1e-06


def padded_2(array, sides, width):
    for axis, dim in sides:
        size, length = (lax.axis_size(axis), array.shape[dim])
        up = [(i, (i + 1) % size) for i in range(size - 1)]
        down = [(j, i) for i, j in up]
        last = lax.slice_in_dim(array, length - width, length, axis=dim)
        first = lax.slice_in_dim(array, 0, width, axis=dim)
        before = lax.ppermute(last, axis, up)
        after = lax.ppermute(first, axis, down)
        array = jnp.concatenate([before, array, after], axis=dim)
    return array


def rms_gain(values, gain):
    return values * lax.rsqrt(jnp.mean(values * values, axis=-1, keepdims=True) + EPS) * gain


def project(inputs, weight):
    return jnp.einsum("fqc,cd->fqd", inputs, weight, preferred_element_type=jnp.float32).astype(
        jnp.bfloat16
    )


def conv_rows(haloed, weight):
    total = None
    for tstep in range(weight.shape[0]):
        part = lax.conv_general_dilated(
            haloed[tstep : tstep + 1],
            weight[tstep],
            window_strides=(1, 1),
            padding=((0, 0), (1, 1)),
            dimension_numbers=("NHWC", "HWIO", "NHWC"),
            preferred_element_type=jnp.float32,
        )
        total = part if total is None else total + part
    return total


def upsample_conv(extended, w_up):
    nf, rp, ncols, chans = extended.shape
    nrows = rp - 2
    outs = w_up.shape[-1]
    padded = jnp.pad(extended, ((0, 0), (0, 0), (1, 1), (0, 0)))
    taps = jnp.einsum(
        "frwc,ijco->frwijo", padded, w_up, preferred_element_type=jnp.float32
    )
    phases_a = []
    for a in range(2):
        phases_b = []
        for b in range(2):
            acc = None
            for dr in range(3):
                ro = (a + dr + 1) // 2
                for dc in range(3):
                    co = (b + dc + 1) // 2
                    term = taps[:, ro : ro + nrows, co : co + ncols, dr, dc, :]
                    acc = term if acc is None else acc + term
            phases_b.append(acc)
        phases_a.append(jnp.stack(phases_b, axis=3))
    result = jnp.stack(phases_a, axis=2)
    return result.astype(jnp.bfloat16).reshape(nf, 2 * nrows, 2 * ncols * outs)


def body(
    frames, norm_attn, w_query, w_key, w_value, w_out, cache_one, norm_conv, conv_weight, w_up
):
    nframes, nrows, ncols, chans = frames.shape
    scale = chans ** (-0.5)

    cache_haloed = padded_2(cache_one, (("rows", 1),), 1)
    cache_part = conv_rows(cache_haloed, conv_weight[:2])

    flat = frames.reshape(nframes, nrows * ncols, chans)
    normed = rms_gain(flat.astype(jnp.float32), norm_attn).astype(jnp.bfloat16)
    normed_all = lax.all_gather(
        normed.reshape(nframes, nrows, ncols, chans), "rows", axis=1, tiled=True
    ).reshape(nframes, -1, chans)
    queries = project(normed, w_query)
    keys = project(normed_all, w_key)
    values = project(normed_all, w_value)
    scores = jnp.einsum("fqc,fkc->fqk", queries, keys, preferred_element_type=jnp.float32) * scale
    top = jnp.max(scores, axis=-1, keepdims=True)
    expo = jnp.exp(scores - top)
    denom = jnp.sum(expo, axis=-1, keepdims=True)
    numer = jnp.einsum(
        "fqk,fkc->fqc", expo.astype(jnp.bfloat16), values, preferred_element_type=jnp.float32
    )
    attended = (numer / denom).astype(jnp.bfloat16)
    mixed = (
        flat.astype(jnp.float32)
        + jnp.einsum("fqc,cd->fqd", attended, w_out, preferred_element_type=jnp.float32)
    ).astype(jnp.bfloat16)
    activ = (
        jax.nn.silu(rms_gain(mixed.astype(jnp.float32), norm_conv))
        .astype(jnp.bfloat16)
        .reshape(nframes, nrows, ncols, chans)
    )
    activ_haloed = padded_2(activ, (("rows", 1),), 1)
    conv_out = (cache_part + conv_rows(activ_haloed, conv_weight[2:])).astype(jnp.bfloat16)
    extended = padded_2(conv_out, (("rows", 1),), 1)
    return upsample_conv(extended, w_up)


def solution(mesh):
    placed = (
        P("clips", "rows", None, None),
        P(),
        P(),
        P(),
        P(),
        P(),
        P("clips", "rows", None, None),
        P(),
        P(),
        P(),
    )
    return jax.shard_map(
        body, mesh=mesh, in_specs=placed, out_specs=P("clips", "rows", None), check_vma=False
    )
```

```python
import jax
import jax.numpy as jnp
from jax import lax
from jax.sharding import PartitionSpec as P

EPS = 1e-06


ROWS = ("chip", "core")


def padded_2(array, sides, width):
    for axis, dim in sides:
        size, length = (lax.axis_size(axis), array.shape[dim])
        up = [(i, (i + 1) % size) for i in range(size - 1)]
        down = [(j, i) for i, j in up]
        last = lax.slice_in_dim(array, length - width, length, axis=dim)
        first = lax.slice_in_dim(array, 0, width, axis=dim)
        before = lax.ppermute(last, axis, up)
        after = lax.ppermute(first, axis, down)
        array = jnp.concatenate([before, array, after], axis=dim)
    return array


def rms_gain(values, gain):
    return values * lax.rsqrt(jnp.mean(values * values, axis=-1, keepdims=True) + EPS) * gain


def project(inputs, weight):
    return jnp.einsum("fqc,cd->fqd", inputs, weight, preferred_element_type=jnp.float32).astype(
        jnp.bfloat16
    )


def conv_rows(haloed, weight):
    total = None
    for tstep in range(weight.shape[0]):
        part = lax.conv_general_dilated(
            haloed[tstep : tstep + 1],
            weight[tstep],
            window_strides=(1, 1),
            padding=((0, 0), (1, 1)),
            dimension_numbers=("NHWC", "HWIO", "NHWC"),
            preferred_element_type=jnp.float32,
        )
        total = part if total is None else total + part
    return total


def upsample_conv(extended, w_up):
    nf, rp, ncols, chans = extended.shape
    nrows = rp - 2
    outs = w_up.shape[-1]
    padded = jnp.pad(extended, ((0, 0), (0, 0), (1, 1), (0, 0)))
    taps = jnp.einsum(
        "frwc,ijco->frwijo", padded, w_up, preferred_element_type=jnp.float32
    )
    phases_a = []
    for a in range(2):
        phases_b = []
        for b in range(2):
            acc = None
            for dr in range(3):
                ro = (a + dr + 1) // 2
                for dc in range(3):
                    co = (b + dc + 1) // 2
                    term = taps[:, ro : ro + nrows, co : co + ncols, dr, dc, :]
                    acc = term if acc is None else acc + term
            phases_b.append(acc)
        phases_a.append(jnp.stack(phases_b, axis=3))
    result = jnp.stack(phases_a, axis=2)
    return result.astype(jnp.bfloat16).reshape(nf, 2 * nrows, 2 * ncols * outs)


def body(
    frames, norm_attn, w_query, w_key, w_value, w_out, cache_one, norm_conv, conv_weight, w_up
):
    nframes, nrows, ncols, chans = frames.shape
    scale = chans ** (-0.5)

    cache_haloed = padded_2(cache_one, ((ROWS, 1),), 1)
    cache_part = conv_rows(cache_haloed, conv_weight[:2])

    flat = frames.reshape(nframes, nrows * ncols, chans)
    normed = rms_gain(flat.astype(jnp.float32), norm_attn).astype(jnp.bfloat16)
    by_chip = lax.all_gather(normed, "chip", axis=1, tiled=True)
    normed_all = lax.all_gather(by_chip, "core", axis=1, tiled=True)
    queries = project(normed, w_query)
    keys = project(normed_all, w_key)
    values = project(normed_all, w_value)
    scores = jnp.einsum("fqc,fkc->fqk", queries, keys, preferred_element_type=jnp.float32) * scale
    top = jnp.max(scores, axis=-1, keepdims=True)
    expo = jnp.exp(scores - top)
    denom = jnp.sum(expo, axis=-1, keepdims=True)
    numer = jnp.einsum(
        "fqk,fkc->fqc", expo.astype(jnp.bfloat16), values, preferred_element_type=jnp.float32
    )
    attended = (numer / denom).astype(jnp.bfloat16)
    mixed = (
        flat.astype(jnp.float32)
        + jnp.einsum("fqc,cd->fqd", attended, w_out, preferred_element_type=jnp.float32)
    ).astype(jnp.bfloat16)
    activ = (
        jax.nn.silu(rms_gain(mixed.astype(jnp.float32), norm_conv))
        .astype(jnp.bfloat16)
        .reshape(nframes, nrows, ncols, chans)
    )
    activ_haloed = padded_2(activ, ((ROWS, 1),), 1)
    conv_out = (cache_part + conv_rows(activ_haloed, conv_weight[2:])).astype(jnp.bfloat16)
    extended = padded_2(conv_out, ((ROWS, 1),), 1)
    return upsample_conv(extended, w_up)


def solution(mesh):
    clips, rows = mesh.devices.shape
    mesh = jax.sharding.Mesh(mesh.devices.reshape(clips, rows // 2, 2), ("clips",) + ROWS)
    placed = (
        P("clips", ROWS, None, None),
        P(),
        P(),
        P(),
        P(),
        P(),
        P("clips", ROWS, None, None),
        P(),
        P(),
        P(),
    )
    return jax.shard_map(
        body, mesh=mesh, in_specs=placed, out_specs=P("clips", ROWS, None), check_vma=False
    )
```

```python
import jax
import jax.numpy as jnp
from jax import lax
from jax.sharding import PartitionSpec as P

EPS = 1e-06


ROWS = ("chip", "core")


def padded_2(array, sides, width):
    for axis, dim in sides:
        size, length = (lax.axis_size(axis), array.shape[dim])
        up = [(i, (i + 1) % size) for i in range(size - 1)]
        down = [(j, i) for i, j in up]
        last = lax.slice_in_dim(array, length - width, length, axis=dim)
        first = lax.slice_in_dim(array, 0, width, axis=dim)
        before = lax.ppermute(last, axis, up)
        after = lax.ppermute(first, axis, down)
        array = jnp.concatenate([before, array, after], axis=dim)
    return array


def rms_gain(values, gain):
    return values * lax.rsqrt(jnp.mean(values * values, axis=-1, keepdims=True) + EPS) * gain


def project(inputs, weight):
    return jnp.einsum("fqc,cd->fqd", inputs, weight, preferred_element_type=jnp.float32).astype(
        jnp.bfloat16
    )


def conv_rows(haloed, weight):
    total = None
    for tstep in range(weight.shape[0]):
        part = lax.conv_general_dilated(
            haloed[tstep : tstep + 1],
            weight[tstep],
            window_strides=(1, 1),
            padding=((0, 0), (1, 1)),
            dimension_numbers=("NHWC", "HWIO", "NHWC"),
            preferred_element_type=jnp.float32,
        )
        total = part if total is None else total + part
    return total


def upsample_conv(extended, w_up):
    nf, rp, ncols, chans = extended.shape
    nrows = rp - 2
    outs = w_up.shape[-1]
    padded = jnp.pad(extended, ((0, 0), (0, 0), (1, 1), (0, 0)))
    taps = jnp.einsum(
        "frwc,ijco->frwijo", padded, w_up, preferred_element_type=jnp.float32
    )
    phases_a = []
    for a in range(2):
        phases_b = []
        for b in range(2):
            acc = None
            for dr in range(3):
                ro = (a + dr + 1) // 2
                for dc in range(3):
                    co = (b + dc + 1) // 2
                    term = taps[:, ro : ro + nrows, co : co + ncols, dr, dc, :]
                    acc = term if acc is None else acc + term
            phases_b.append(acc)
        phases_a.append(jnp.stack(phases_b, axis=3))
    result = jnp.stack(phases_a, axis=2)
    return result.astype(jnp.bfloat16).reshape(nf, 2 * nrows, 2 * ncols * outs)


def body(
    frames, norm_attn, w_query, w_key, w_value, w_out, cache_one, norm_conv, conv_weight, w_up
):
    nframes, nrows, ncols, chans = frames.shape
    scale = chans ** (-0.5)

    cache_haloed = padded_2(cache_one, ((ROWS, 1),), 1)
    cache_part = conv_rows(cache_haloed, conv_weight[:2])

    flat = frames.reshape(nframes, nrows * ncols, chans)
    normed = rms_gain(flat.astype(jnp.float32), norm_attn).astype(jnp.bfloat16)
    queries = project(normed, w_query)
    size = lax.axis_size(ROWS)
    pieces, held, bit = [normed], normed, size // 2
    while bit >= 1:
        other = lax.ppermute(held, ROWS, [(i, i ^ bit) for i in range(size)])
        pieces.append(other)
        if bit > 1:
            held = jnp.concatenate([held, other], axis=1)
        bit //= 2
    scores, values = [], []
    for piece in pieces:
        keys = project(piece, w_key)
        values.append(project(piece, w_value))
        scores.append(
            jnp.einsum("fqc,fkc->fqk", queries, keys, preferred_element_type=jnp.float32) * scale
        )
    top = jnp.max(jnp.stack([jnp.max(s, axis=-1) for s in scores], axis=-1), axis=-1)[..., None]
    expos = [jnp.exp(s - top) for s in scores]
    denom = sum(jnp.sum(e, axis=-1, keepdims=True) for e in expos)
    numer = sum(
        jnp.einsum("fqk,fkc->fqc", e.astype(jnp.bfloat16), v, preferred_element_type=jnp.float32)
        for e, v in zip(expos, values)
    )
    attended = (numer / denom).astype(jnp.bfloat16)
    mixed = (
        flat.astype(jnp.float32)
        + jnp.einsum("fqc,cd->fqd", attended, w_out, preferred_element_type=jnp.float32)
    ).astype(jnp.bfloat16)
    activ = (
        jax.nn.silu(rms_gain(mixed.astype(jnp.float32), norm_conv))
        .astype(jnp.bfloat16)
        .reshape(nframes, nrows, ncols, chans)
    )
    activ_haloed = padded_2(activ, ((ROWS, 1),), 1)
    conv_out = (cache_part + conv_rows(activ_haloed, conv_weight[2:])).astype(jnp.bfloat16)
    extended = padded_2(conv_out, ((ROWS, 1),), 1)
    return upsample_conv(extended, w_up)


def solution(mesh):
    clips, rows = mesh.devices.shape
    mesh = jax.sharding.Mesh(mesh.devices.reshape(clips, rows // 2, 2), ("clips",) + ROWS)
    placed = (
        P("clips", ROWS, None, None),
        P(),
        P(),
        P(),
        P(),
        P(),
        P("clips", ROWS, None, None),
        P(),
        P(),
        P(),
    )
    return jax.shard_map(
        body, mesh=mesh, in_specs=placed, out_specs=P("clips", ROWS, None), check_vma=False
    )
```

```python
import jax
import jax.numpy as jnp
from jax import lax
from jax.sharding import PartitionSpec as P

EPS = 1e-06


ROWS = ("chip", "core")


def padded_2(array, sides, width):
    for axis, dim in sides:
        size, length = (lax.axis_size(axis), array.shape[dim])
        up = [(i, (i + 1) % size) for i in range(size - 1)]
        down = [(j, i) for i, j in up]
        last = lax.slice_in_dim(array, length - width, length, axis=dim)
        first = lax.slice_in_dim(array, 0, width, axis=dim)
        before = lax.ppermute(last, axis, up)
        after = lax.ppermute(first, axis, down)
        array = jnp.concatenate([before, array, after], axis=dim)
    return array


def rms_gain(values, gain):
    return values * lax.rsqrt(jnp.mean(values * values, axis=-1, keepdims=True) + EPS) * gain


def project(inputs, weight):
    return jnp.einsum("fqc,cd->fqd", inputs, weight, preferred_element_type=jnp.float32).astype(
        jnp.bfloat16
    )


def conv_rows(haloed, weight):
    total = None
    for tstep in range(weight.shape[0]):
        part = lax.conv_general_dilated(
            haloed[tstep : tstep + 1],
            weight[tstep],
            window_strides=(1, 1),
            padding=((0, 0), (1, 1)),
            dimension_numbers=("NHWC", "HWIO", "NHWC"),
            preferred_element_type=jnp.float32,
        )
        total = part if total is None else total + part
    return total


def upsample_conv(extended, w_up):
    nf, rp, ncols, chans = extended.shape
    nrows = rp - 2
    outs = w_up.shape[-1]
    padded = jnp.pad(extended, ((0, 0), (0, 0), (1, 1), (0, 0)))
    taps = jnp.einsum(
        "frwc,ijco->frwijo", padded, w_up, preferred_element_type=jnp.float32
    )
    phases_a = []
    for a in range(2):
        phases_b = []
        for b in range(2):
            acc = None
            for dr in range(3):
                ro = (a + dr + 1) // 2
                for dc in range(3):
                    co = (b + dc + 1) // 2
                    term = taps[:, ro : ro + nrows, co : co + ncols, dr, dc, :]
                    acc = term if acc is None else acc + term
            phases_b.append(acc)
        phases_a.append(jnp.stack(phases_b, axis=3))
    result = jnp.stack(phases_a, axis=2)
    return result.astype(jnp.bfloat16).reshape(nf, 2 * nrows, 2 * ncols * outs)


def body(
    frames, norm_attn, w_query, w_key, w_value, w_out, cache_one, norm_conv, conv_weight, w_up
):
    nframes, nrows, ncols, chans = frames.shape
    scale = chans ** (-0.5)

    cache_haloed = padded_2(cache_one, ((ROWS, 1),), 1)
    cache_part = conv_rows(cache_haloed, conv_weight[:2])

    flat = frames.reshape(nframes, nrows * ncols, chans)
    normed = rms_gain(flat.astype(jnp.float32), norm_attn).astype(jnp.bfloat16)
    queries = project(normed, w_query)
    size = lax.axis_size(ROWS)
    chip_bits = [1 << k for k in range(1, size.bit_length() - 1)][::-1]
    orders = (chip_bits, chip_bits[-1:] + chip_bits[:-1])
    mine, held = [normed], normed
    for step in range(len(chip_bits)):
        perm = [(i, i ^ orders[i & 1][step]) for i in range(size)]
        other = lax.ppermute(held, ROWS, perm)
        mine.append(other)
        if step + 1 < len(chip_bits):
            held = jnp.concatenate([held, other], axis=1)
    swap = [(i, i ^ 1) for i in range(size)]
    pieces = mine + [lax.ppermute(piece, ROWS, swap) for piece in mine]
    scores, values = [], []
    for piece in pieces:
        keys = project(piece, w_key)
        values.append(project(piece, w_value))
        scores.append(
            jnp.einsum("fqc,fkc->fqk", queries, keys, preferred_element_type=jnp.float32) * scale
        )
    top = jnp.max(jnp.stack([jnp.max(s, axis=-1) for s in scores], axis=-1), axis=-1)[..., None]
    expos = [jnp.exp(s - top) for s in scores]
    denom = sum(jnp.sum(e, axis=-1, keepdims=True) for e in expos)
    numer = sum(
        jnp.einsum("fqk,fkc->fqc", e.astype(jnp.bfloat16), v, preferred_element_type=jnp.float32)
        for e, v in zip(expos, values)
    )
    attended = (numer / denom).astype(jnp.bfloat16)
    mixed = (
        flat.astype(jnp.float32)
        + jnp.einsum("fqc,cd->fqd", attended, w_out, preferred_element_type=jnp.float32)
    ).astype(jnp.bfloat16)
    activ = (
        jax.nn.silu(rms_gain(mixed.astype(jnp.float32), norm_conv))
        .astype(jnp.bfloat16)
        .reshape(nframes, nrows, ncols, chans)
    )
    activ_haloed = padded_2(activ, ((ROWS, 1),), 1)
    conv_out = (cache_part + conv_rows(activ_haloed, conv_weight[2:])).astype(jnp.bfloat16)
    extended = padded_2(conv_out, ((ROWS, 1),), 1)
    return upsample_conv(extended, w_up)


def solution(mesh):
    clips, rows = mesh.devices.shape
    mesh = jax.sharding.Mesh(mesh.devices.reshape(clips, rows // 2, 2), ("clips",) + ROWS)
    placed = (
        P("clips", ROWS, None, None),
        P(),
        P(),
        P(),
        P(),
        P(),
        P("clips", ROWS, None, None),
        P(),
        P(),
        P(),
    )
    return jax.shard_map(
        body, mesh=mesh, in_specs=placed, out_specs=P("clips", ROWS, None), check_vma=False
    )
```

```python
import jax
import jax.numpy as jnp
from jax import lax
from jax.sharding import PartitionSpec as P

EPS = 1e-06


ROWS = ("chip", "core")


def padded_2(array, sides, width):
    for axis, dim in sides:
        size, length = (lax.axis_size(axis), array.shape[dim])
        up = [(i, (i + 1) % size) for i in range(size - 1)]
        down = [(j, i) for i, j in up]
        last = lax.slice_in_dim(array, length - width, length, axis=dim)
        first = lax.slice_in_dim(array, 0, width, axis=dim)
        before = lax.ppermute(last, axis, up)
        after = lax.ppermute(first, axis, down)
        array = jnp.concatenate([before, array, after], axis=dim)
    return array


def rms_gain(values, gain):
    return values * lax.rsqrt(jnp.mean(values * values, axis=-1, keepdims=True) + EPS) * gain


def project(inputs, weight):
    return jnp.einsum("fqc,cd->fqd", inputs, weight, preferred_element_type=jnp.float32).astype(
        jnp.bfloat16
    )


def split_pair(values, axis):
    high = values.astype(jnp.bfloat16)
    low = (values - high.astype(jnp.float32)).astype(jnp.bfloat16)
    return jnp.concatenate([high, low], axis=axis)


def conv_rows(haloed, weight):
    total = None
    for tstep in range(weight.shape[0]):
        part = lax.conv_general_dilated(
            haloed[tstep : tstep + 1],
            weight[tstep],
            window_strides=(1, 1),
            padding=((0, 0), (1, 1)),
            dimension_numbers=("NHWC", "HWIO", "NHWC"),
            preferred_element_type=jnp.float32,
        )
        total = part if total is None else total + part
    return total


def upsample_conv(extended, w_up):
    nf, rp, ncols, chans = extended.shape
    nrows = rp - 2
    outs = w_up.shape[-1]
    padded = jnp.pad(extended, ((0, 0), (0, 0), (1, 1), (0, 0)))
    taps = jnp.einsum(
        "frwc,ijco->frwijo", padded, w_up, preferred_element_type=jnp.float32
    )
    phases_a = []
    for a in range(2):
        phases_b = []
        for b in range(2):
            acc = None
            for dr in range(3):
                ro = (a + dr + 1) // 2
                for dc in range(3):
                    co = (b + dc + 1) // 2
                    term = taps[:, ro : ro + nrows, co : co + ncols, dr, dc, :]
                    acc = term if acc is None else acc + term
            phases_b.append(acc)
        phases_a.append(jnp.stack(phases_b, axis=3))
    result = jnp.stack(phases_a, axis=2)
    return result.astype(jnp.bfloat16).reshape(nf, 2 * nrows, 2 * ncols * outs)


def body(
    frames, norm_attn, w_query, w_key, w_value, w_out, cache_one, norm_conv, conv_weight, w_up
):
    nframes, nrows, ncols, chans = frames.shape
    scale = chans ** (-0.5)

    cache_haloed = padded_2(cache_one, ((ROWS, 1),), 1)
    cache_part = conv_rows(cache_haloed, conv_weight[:2])

    flat = frames.reshape(nframes, nrows * ncols, chans)
    normed = rms_gain(flat.astype(jnp.float32), norm_attn).astype(jnp.bfloat16)
    queries = project(normed, w_query)
    size = lax.axis_size(ROWS)
    chip_bits = [1 << k for k in range(1, size.bit_length() - 1)][::-1]
    orders = (chip_bits, chip_bits[-1:] + chip_bits[:-1])
    mine, held = [normed], normed
    for step in range(len(chip_bits)):
        perm = [(i, i ^ orders[i & 1][step]) for i in range(size)]
        other = lax.ppermute(held, ROWS, perm)
        mine.append(other)
        if step + 1 < len(chip_bits):
            held = jnp.concatenate([held, other], axis=1)
    swap = [(i, i ^ 1) for i in range(size)]
    pieces = mine + [lax.ppermute(piece, ROWS, swap) for piece in mine]
    q_keyed = jnp.einsum("fqc,dc->fqd", queries, w_key, preferred_element_type=jnp.float32)
    q_pair = split_pair(q_keyed, axis=1)
    count = queries.shape[1]
    scores = []
    for piece in pieces:
        both = jnp.einsum("fqc,fkc->fqk", q_pair, piece, preferred_element_type=jnp.float32)
        scores.append((both[:, :count] + both[:, count:]) * scale)
    top = jnp.max(jnp.stack([jnp.max(s, axis=-1) for s in scores], axis=-1), axis=-1)[..., None]
    expos = [jnp.exp(s - top) for s in scores]
    denom = sum(jnp.sum(e, axis=-1, keepdims=True) for e in expos)
    mixed_in = sum(
        jnp.einsum("fqk,fkc->fqc", e.astype(jnp.bfloat16), p, preferred_element_type=jnp.float32)
        for e, p in zip(expos, pieces)
    )
    both = jnp.einsum(
        "fqc,cd->fqd", split_pair(mixed_in, axis=1), w_value, preferred_element_type=jnp.float32
    )
    numer = both[:, :count] + both[:, count:]
    attended = (numer / denom).astype(jnp.bfloat16)
    mixed = (
        flat.astype(jnp.float32)
        + jnp.einsum("fqc,cd->fqd", attended, w_out, preferred_element_type=jnp.float32)
    ).astype(jnp.bfloat16)
    activ = (
        jax.nn.silu(rms_gain(mixed.astype(jnp.float32), norm_conv))
        .astype(jnp.bfloat16)
        .reshape(nframes, nrows, ncols, chans)
    )
    activ_haloed = padded_2(activ, ((ROWS, 1),), 1)
    conv_out = (cache_part + conv_rows(activ_haloed, conv_weight[2:])).astype(jnp.bfloat16)
    extended = padded_2(conv_out, ((ROWS, 1),), 1)
    return upsample_conv(extended, w_up)


def solution(mesh):
    clips, rows = mesh.devices.shape
    mesh = jax.sharding.Mesh(mesh.devices.reshape(clips, rows // 2, 2), ("clips",) + ROWS)
    placed = (
        P("clips", ROWS, None, None),
        P(),
        P(),
        P(),
        P(),
        P(),
        P("clips", ROWS, None, None),
        P(),
        P(),
        P(),
    )
    return jax.shard_map(
        body, mesh=mesh, in_specs=placed, out_specs=P("clips", ROWS, None), check_vma=False
    )
```

```python
import jax
import jax.numpy as jnp
from jax import lax
from jax.sharding import PartitionSpec as P

EPS = 1e-06


ROWS = ("chip", "core")


def padded_2(array, sides, width):
    for axis, dim in sides:
        size, length = (lax.axis_size(axis), array.shape[dim])
        up = [(i, (i + 1) % size) for i in range(size - 1)]
        down = [(j, i) for i, j in up]
        last = lax.slice_in_dim(array, length - width, length, axis=dim)
        first = lax.slice_in_dim(array, 0, width, axis=dim)
        before = lax.ppermute(last, axis, up)
        after = lax.ppermute(first, axis, down)
        array = jnp.concatenate([before, array, after], axis=dim)
    return array


def rms_gain(values, gain):
    return values * lax.rsqrt(jnp.mean(values * values, axis=-1, keepdims=True) + EPS) * gain


def project(inputs, weight):
    return jnp.einsum("fqc,cd->fqd", inputs, weight, preferred_element_type=jnp.float32).astype(
        jnp.bfloat16
    )


def split_pair(values, axis):
    high = values.astype(jnp.bfloat16)
    low = (values - high.astype(jnp.float32)).astype(jnp.bfloat16)
    return jnp.concatenate([high, low], axis=axis)


def conv_rows(haloed, weight):
    total = None
    for tstep in range(weight.shape[0]):
        part = lax.conv_general_dilated(
            haloed[tstep : tstep + 1],
            weight[tstep],
            window_strides=(1, 1),
            padding=((0, 0), (1, 1)),
            dimension_numbers=("NHWC", "HWIO", "NHWC"),
            preferred_element_type=jnp.float32,
        )
        total = part if total is None else total + part
    return total


def upsample_conv(extended, w_up):
    nf, rp, ncols, chans = extended.shape
    nrows = rp - 2
    outs = w_up.shape[-1]
    padded = jnp.pad(extended, ((0, 0), (0, 0), (1, 1), (0, 0)))
    taps = jnp.einsum(
        "frwc,ijco->frwijo", padded, w_up, preferred_element_type=jnp.float32
    )
    phases_a = []
    for a in range(2):
        phases_b = []
        for b in range(2):
            acc = None
            for dr in range(3):
                ro = (a + dr + 1) // 2
                for dc in range(3):
                    co = (b + dc + 1) // 2
                    term = taps[:, ro : ro + nrows, co : co + ncols, dr, dc, :]
                    acc = term if acc is None else acc + term
            phases_b.append(acc)
        phases_a.append(jnp.stack(phases_b, axis=3))
    result = jnp.stack(phases_a, axis=2)
    return result.astype(jnp.bfloat16).reshape(nf, 2 * nrows, 2 * ncols * outs)


def body(
    frames, norm_attn, w_query, w_key, w_value, w_out, cache_one, norm_conv, conv_weight, w_up
):
    nframes, nrows, ncols, chans = frames.shape
    scale = chans ** (-0.5)

    cache_haloed = padded_2(cache_one, ((ROWS, 1),), 2)
    cache_part = conv_rows(cache_haloed, conv_weight[:2])

    flat = frames.reshape(nframes, nrows * ncols, chans)
    normed = rms_gain(flat.astype(jnp.float32), norm_attn).astype(jnp.bfloat16)
    queries = project(normed, w_query)
    size = lax.axis_size(ROWS)
    chip_bits = [1 << k for k in range(1, size.bit_length() - 1)][::-1]
    orders = (chip_bits, chip_bits[-1:] + chip_bits[:-1])
    mine, held = [normed], normed
    for step in range(len(chip_bits)):
        perm = [(i, i ^ orders[i & 1][step]) for i in range(size)]
        other = lax.ppermute(held, ROWS, perm)
        mine.append(other)
        if step + 1 < len(chip_bits):
            held = jnp.concatenate([held, other], axis=1)
    swap = [(i, i ^ 1) for i in range(size)]
    pieces = mine + [lax.ppermute(piece, ROWS, swap) for piece in mine]
    q_keyed = jnp.einsum("fqc,dc->fqd", queries, w_key, preferred_element_type=jnp.float32)
    q_pair = split_pair(q_keyed, axis=1)
    count = queries.shape[1]
    scores = []
    for piece in pieces:
        both = jnp.einsum("fqc,fkc->fqk", q_pair, piece, preferred_element_type=jnp.float32)
        scores.append((both[:, :count] + both[:, count:]) * scale)
    top = jnp.max(jnp.stack([jnp.max(s, axis=-1) for s in scores], axis=-1), axis=-1)[..., None]
    expos = [jnp.exp(s - top) for s in scores]
    denom = sum(jnp.sum(e, axis=-1, keepdims=True) for e in expos)
    mixed_in = sum(
        jnp.einsum("fqk,fkc->fqc", e.astype(jnp.bfloat16), p, preferred_element_type=jnp.float32)
        for e, p in zip(expos, pieces)
    )
    both = jnp.einsum(
        "fqc,cd->fqd", split_pair(mixed_in, axis=1), w_value, preferred_element_type=jnp.float32
    )
    numer = both[:, :count] + both[:, count:]
    attended = (numer / denom).astype(jnp.bfloat16)
    mixed = (
        flat.astype(jnp.float32)
        + jnp.einsum("fqc,cd->fqd", attended, w_out, preferred_element_type=jnp.float32)
    ).astype(jnp.bfloat16)
    activ = (
        jax.nn.silu(rms_gain(mixed.astype(jnp.float32), norm_conv))
        .astype(jnp.bfloat16)
        .reshape(nframes, nrows, ncols, chans)
    )
    activ_haloed = padded_2(activ, ((ROWS, 1),), 2)
    extended = cache_part + conv_rows(activ_haloed, conv_weight[2:])
    where = lax.axis_index(ROWS)
    line = jnp.arange(nrows + 2)
    inside = ((line > 0) | (where > 0)) & ((line < nrows + 1) | (where < size - 1))
    extended = jnp.where(inside[None, :, None, None], extended, 0.0).astype(jnp.bfloat16)
    return upsample_conv(extended, w_up)


def solution(mesh):
    clips, rows = mesh.devices.shape
    mesh = jax.sharding.Mesh(mesh.devices.reshape(clips, rows // 2, 2), ("clips",) + ROWS)
    placed = (
        P("clips", ROWS, None, None),
        P(),
        P(),
        P(),
        P(),
        P(),
        P("clips", ROWS, None, None),
        P(),
        P(),
        P(),
    )
    return jax.shard_map(
        body, mesh=mesh, in_specs=placed, out_specs=P("clips", ROWS, None), check_vma=False
    )
```

```python
import jax
import jax.numpy as jnp
from jax import lax
from jax.sharding import PartitionSpec as P

EPS = 1e-06


ROWS = ("chip", "core")


def padded_2(array, sides, width):
    for axis, dim in sides:
        size, length = (lax.axis_size(axis), array.shape[dim])
        up = [(i, (i + 1) % size) for i in range(size - 1)]
        down = [(j, i) for i, j in up]
        last = lax.slice_in_dim(array, length - width, length, axis=dim)
        first = lax.slice_in_dim(array, 0, width, axis=dim)
        before = lax.ppermute(last, axis, up)
        after = lax.ppermute(first, axis, down)
        array = jnp.concatenate([before, array, after], axis=dim)
    return array


def rms_gain(values, gain):
    return values * lax.rsqrt(jnp.mean(values * values, axis=-1, keepdims=True) + EPS) * gain


def project(inputs, weight):
    return jnp.einsum("fqc,cd->fqd", inputs, weight, preferred_element_type=jnp.float32).astype(
        jnp.bfloat16
    )


def exchange(values, bits, size):
    masks = [0]
    for bit in bits:
        masks = masks + [mask | bit for mask in masks]
    return [
        lax.ppermute(values, ROWS, [(i, i ^ mask) for i in range(size)]) for mask in masks[1:]
    ]


def split_pair(values, axis):
    high = values.astype(jnp.bfloat16)
    low = (values - high.astype(jnp.float32)).astype(jnp.bfloat16)
    return jnp.concatenate([high, low], axis=axis)


def conv_rows(haloed, weight):
    total = None
    for tstep in range(weight.shape[0]):
        part = lax.conv_general_dilated(
            haloed[tstep : tstep + 1],
            weight[tstep],
            window_strides=(1, 1),
            padding=((0, 0), (1, 1)),
            dimension_numbers=("NHWC", "HWIO", "NHWC"),
            preferred_element_type=jnp.float32,
        )
        total = part if total is None else total + part
    return total


def upsample_conv(extended, w_up):
    nf, rp, ncols, chans = extended.shape
    nrows = rp - 2
    outs = w_up.shape[-1]
    padded = jnp.pad(extended, ((0, 0), (0, 0), (1, 1), (0, 0)))
    taps = jnp.einsum(
        "frwc,ijco->frwijo", padded, w_up, preferred_element_type=jnp.float32
    )
    phases_a = []
    for a in range(2):
        phases_b = []
        for b in range(2):
            acc = None
            for dr in range(3):
                ro = (a + dr + 1) // 2
                for dc in range(3):
                    co = (b + dc + 1) // 2
                    term = taps[:, ro : ro + nrows, co : co + ncols, dr, dc, :]
                    acc = term if acc is None else acc + term
            phases_b.append(acc)
        phases_a.append(jnp.stack(phases_b, axis=3))
    result = jnp.stack(phases_a, axis=2)
    return result.astype(jnp.bfloat16).reshape(nf, 2 * nrows, 2 * ncols * outs)


def body(
    frames, norm_attn, w_query, w_key, w_value, w_out, cache_one, norm_conv, conv_weight, w_up
):
    nframes, nrows, ncols, chans = frames.shape
    scale = chans ** (-0.5)

    cache_haloed = padded_2(cache_one, ((ROWS, 1),), 1)
    cache_part = conv_rows(cache_haloed, conv_weight[:2])

    flat = frames.reshape(nframes, nrows * ncols, chans)
    normed = rms_gain(flat.astype(jnp.float32), norm_attn).astype(jnp.bfloat16)
    queries = project(normed, w_query)
    size = lax.axis_size(ROWS)
    chip_bits = [1 << k for k in range(1, size.bit_length() - 1)]
    low, high = chip_bits[:1], chip_bits[1:]
    half = normed.shape[1] // 2
    first, second = normed[:, :half], normed[:, half:]
    first_in = exchange(first, high, size)
    second_in = exchange(second, low, size)
    gathered = jnp.concatenate([first, second] + first_in + second_in, axis=1)
    first_out = exchange(jnp.concatenate([first] + first_in, axis=1), low, size)
    second_out = exchange(jnp.concatenate([second] + second_in, axis=1), high, size)
    mine = [gathered] + first_out + second_out
    pieces = mine + [exchange(piece, [1], size)[0] for piece in mine]
    q_keyed = jnp.einsum("fqc,dc->fqd", queries, w_key, preferred_element_type=jnp.float32)
    q_pair = split_pair(q_keyed, axis=1)
    count = queries.shape[1]
    scores = []
    for piece in pieces:
        both = jnp.einsum("fqc,fkc->fqk", q_pair, piece, preferred_element_type=jnp.float32)
        scores.append((both[:, :count] + both[:, count:]) * scale)
    top = jnp.max(jnp.stack([jnp.max(s, axis=-1) for s in scores], axis=-1), axis=-1)[..., None]
    expos = [jnp.exp(s - top) for s in scores]
    denom = sum(jnp.sum(e, axis=-1, keepdims=True) for e in expos)
    mixed_in = sum(
        jnp.einsum("fqk,fkc->fqc", e.astype(jnp.bfloat16), p, preferred_element_type=jnp.float32)
        for e, p in zip(expos, pieces)
    )
    both = jnp.einsum(
        "fqc,cd->fqd", split_pair(mixed_in, axis=1), w_value, preferred_element_type=jnp.float32
    )
    numer = both[:, :count] + both[:, count:]
    attended = (numer / denom).astype(jnp.bfloat16)
    mixed = (
        flat.astype(jnp.float32)
        + jnp.einsum("fqc,cd->fqd", attended, w_out, preferred_element_type=jnp.float32)
    ).astype(jnp.bfloat16)
    activ = (
        jax.nn.silu(rms_gain(mixed.astype(jnp.float32), norm_conv))
        .astype(jnp.bfloat16)
        .reshape(nframes, nrows, ncols, chans)
    )
    activ_haloed = padded_2(activ, ((ROWS, 1),), 1)
    conv_out = (cache_part + conv_rows(activ_haloed, conv_weight[2:])).astype(jnp.bfloat16)
    extended = padded_2(conv_out, ((ROWS, 1),), 1)
    return upsample_conv(extended, w_up)


def solution(mesh):
    clips, rows = mesh.devices.shape
    mesh = jax.sharding.Mesh(mesh.devices.reshape(clips, rows // 2, 2), ("clips",) + ROWS)
    placed = (
        P("clips", ROWS, None, None),
        P(),
        P(),
        P(),
        P(),
        P(),
        P("clips", ROWS, None, None),
        P(),
        P(),
        P(),
    )
    return jax.shard_map(
        body, mesh=mesh, in_specs=placed, out_specs=P("clips", ROWS, None), check_vma=False
    )
```

```python
import jax
import jax.numpy as jnp
from jax import lax
from jax.sharding import PartitionSpec as P

EPS = 1e-06


ROWS = ("chip", "core")


def padded_2(array, sides, width):
    for axis, dim in sides:
        size, length = (lax.axis_size(axis), array.shape[dim])
        up = [(i, (i + 1) % size) for i in range(size - 1)]
        down = [(j, i) for i, j in up]
        last = lax.slice_in_dim(array, length - width, length, axis=dim)
        first = lax.slice_in_dim(array, 0, width, axis=dim)
        before = lax.ppermute(last, axis, up)
        after = lax.ppermute(first, axis, down)
        array = jnp.concatenate([before, array, after], axis=dim)
    return array


def rms_gain(values, gain):
    return values * lax.rsqrt(jnp.mean(values * values, axis=-1, keepdims=True) + EPS) * gain


def project(inputs, weight):
    return jnp.einsum("fqc,cd->fqd", inputs, weight, preferred_element_type=jnp.float32).astype(
        jnp.bfloat16
    )


def exchange(values, bits, size):
    masks = [0]
    for bit in bits:
        masks = masks + [mask | bit for mask in masks]
    return [
        lax.ppermute(values, ROWS, [(i, i ^ mask) for i in range(size)]) for mask in masks[1:]
    ]


def split_pair(values, axis):
    high = values.astype(jnp.bfloat16)
    low = (values - high.astype(jnp.float32)).astype(jnp.bfloat16)
    return jnp.concatenate([high, low], axis=axis)


def conv_rows(haloed, weight):
    nt, rp, ncols, chans = haloed.shape
    rows_out = rp - 2
    padded = jnp.pad(haloed, ((0, 0), (0, 0), (1, 1), (0, 0)))
    wide = jnp.concatenate([padded[:, :, shift : shift + ncols] for shift in range(3)], axis=-1)
    total = None
    for tstep in range(nt):
        for rstep in range(3):
            part = wide[tstep, rstep : rstep + rows_out].reshape(-1, 3 * chans)
            term = jnp.dot(
                part,
                weight[tstep, rstep].reshape(3 * chans, -1),
                preferred_element_type=jnp.float32,
            )
            total = term if total is None else total + term
    return total.reshape(1, rows_out, ncols, -1)


def upsample_conv(extended, w_up):
    nf, rp, ncols, chans = extended.shape
    nrows = rp - 2
    outs = w_up.shape[-1]
    padded = jnp.pad(extended, ((0, 0), (0, 0), (1, 1), (0, 0)))
    taps = jnp.einsum(
        "frwc,ijco->frwijo", padded, w_up, preferred_element_type=jnp.float32
    )
    phases_a = []
    for a in range(2):
        phases_b = []
        for b in range(2):
            acc = None
            for dr in range(3):
                ro = (a + dr + 1) // 2
                for dc in range(3):
                    co = (b + dc + 1) // 2
                    term = taps[:, ro : ro + nrows, co : co + ncols, dr, dc, :]
                    acc = term if acc is None else acc + term
            phases_b.append(acc)
        phases_a.append(jnp.stack(phases_b, axis=3))
    result = jnp.stack(phases_a, axis=2)
    return result.astype(jnp.bfloat16).reshape(nf, 2 * nrows, 2 * ncols * outs)


def body(
    frames, norm_attn, w_query, w_key, w_value, w_out, cache_one, norm_conv, conv_weight, w_up
):
    nframes, nrows, ncols, chans = frames.shape
    scale = chans ** (-0.5)

    cache_haloed = padded_2(cache_one, ((ROWS, 1),), 2)
    cache_part = conv_rows(cache_haloed, conv_weight[:2])

    flat = frames.reshape(nframes, nrows * ncols, chans)
    normed = rms_gain(flat.astype(jnp.float32), norm_attn).astype(jnp.bfloat16)
    queries = project(normed, w_query)
    size = lax.axis_size(ROWS)
    chip_bits = [1 << k for k in range(1, size.bit_length() - 1)]
    low, high = chip_bits[:1], chip_bits[1:]
    half = normed.shape[1] // 2
    first, second = normed[:, :half], normed[:, half:]
    first_in = exchange(first, high, size)
    second_in = exchange(second, low, size)
    gathered = jnp.concatenate([first, second] + first_in + second_in, axis=1)
    first_out = exchange(jnp.concatenate([first] + first_in, axis=1), low, size)
    second_out = exchange(jnp.concatenate([second] + second_in, axis=1), high, size)
    mine = [gathered] + first_out + second_out
    pieces = mine + [exchange(piece, [1], size)[0] for piece in mine]
    q_keyed = jnp.einsum("fqc,dc->fqd", queries, w_key, preferred_element_type=jnp.float32)
    q_pair = split_pair(q_keyed, axis=1)
    count = queries.shape[1]
    scores = []
    for piece in pieces:
        both = jnp.einsum("fqc,fkc->fqk", q_pair, piece, preferred_element_type=jnp.float32)
        scores.append((both[:, :count] + both[:, count:]) * scale)
    top = jnp.max(jnp.stack([jnp.max(s, axis=-1) for s in scores], axis=-1), axis=-1)[..., None]
    expos = [jnp.exp(s - top) for s in scores]
    denom = sum(jnp.sum(e, axis=-1, keepdims=True) for e in expos)
    mixed_in = sum(
        jnp.einsum("fqk,fkc->fqc", e.astype(jnp.bfloat16), p, preferred_element_type=jnp.float32)
        for e, p in zip(expos, pieces)
    )
    both = jnp.einsum(
        "fqc,cd->fqd", split_pair(mixed_in, axis=1), w_value, preferred_element_type=jnp.float32
    )
    numer = both[:, :count] + both[:, count:]
    attended = (numer / denom).astype(jnp.bfloat16)
    mixed = (
        flat.astype(jnp.float32)
        + jnp.einsum("fqc,cd->fqd", attended, w_out, preferred_element_type=jnp.float32)
    ).astype(jnp.bfloat16)
    activ = (
        jax.nn.silu(rms_gain(mixed.astype(jnp.float32), norm_conv))
        .astype(jnp.bfloat16)
        .reshape(nframes, nrows, ncols, chans)
    )
    activ_haloed = padded_2(activ, ((ROWS, 1),), 2)
    extended = cache_part + conv_rows(activ_haloed, conv_weight[2:])
    where = lax.axis_index(ROWS)
    line = jnp.arange(nrows + 2)
    inside = ((line > 0) | (where > 0)) & ((line < nrows + 1) | (where < size - 1))
    extended = jnp.where(inside[None, :, None, None], extended, 0.0).astype(jnp.bfloat16)
    return upsample_conv(extended, w_up)


def solution(mesh):
    clips, rows = mesh.devices.shape
    mesh = jax.sharding.Mesh(mesh.devices.reshape(clips, rows // 2, 2), ("clips",) + ROWS)
    placed = (
        P("clips", ROWS, None, None),
        P(),
        P(),
        P(),
        P(),
        P(),
        P("clips", ROWS, None, None),
        P(),
        P(),
        P(),
    )
    return jax.shard_map(
        body, mesh=mesh, in_specs=placed, out_specs=P("clips", ROWS, None), check_vma=False
    )
```

```python
import jax
import jax.numpy as jnp
from jax import lax
from jax.sharding import PartitionSpec as P


EPS = 1e-06


ROWS = ("chip", "core")


def padded_2(array, sides, width):
    for axis, dim in sides:
        size, length = (lax.axis_size(axis), array.shape[dim])
        up = [(i, (i + 1) % size) for i in range(size - 1)]
        down = [(j, i) for i, j in up]
        last = lax.slice_in_dim(array, length - width, length, axis=dim)
        first = lax.slice_in_dim(array, 0, width, axis=dim)
        before = lax.ppermute(last, axis, up)
        after = lax.ppermute(first, axis, down)
        array = jnp.concatenate([before, array, after], axis=dim)
    return array


def rms_gain(values, gain):
    return values * lax.rsqrt(jnp.mean(values * values, axis=-1, keepdims=True) + EPS) * gain


def project(inputs, weight):
    return jnp.einsum("fqc,cd->fqd", inputs, weight, preferred_element_type=jnp.float32).astype(
        jnp.bfloat16
    )


def exchange(values, bits, size):
    masks = [0]
    for bit in bits:
        masks = masks + [mask | bit for mask in masks]
    return [
        lax.ppermute(values, ROWS, [(i, i ^ mask) for i in range(size)]) for mask in masks[1:]
    ]


def split_pair(values, axis):
    high = values.astype(jnp.bfloat16)
    low = (values - high.astype(jnp.float32)).astype(jnp.bfloat16)
    return jnp.concatenate([high, low], axis=axis)


def conv_rows(haloed, weight):
    nt, rp, ncols, chans = haloed.shape
    rows_out = rp - 2
    padded = jnp.pad(haloed, ((0, 0), (0, 0), (1, 1), (0, 0)))
    wide = jnp.concatenate([padded[:, :, shift : shift + ncols] for shift in range(3)], axis=-1)
    total = None
    for tstep in range(nt):
        for rstep in range(3):
            part = wide[tstep, rstep : rstep + rows_out].reshape(-1, 3 * chans)
            term = jnp.dot(
                part,
                weight[tstep, rstep].reshape(3 * chans, -1),
                preferred_element_type=jnp.float32,
            )
            total = term if total is None else total + term
    return total.reshape(1, rows_out, ncols, -1)


def upsample_conv(extended, w_up):
    nf, rp, ncols, _ = extended.shape
    nrows = rp - 2
    outs = w_up.shape[-1]
    padded = jnp.pad(extended, ((0, 0), (0, 0), (1, 1), (0, 0)))
    taps = jnp.einsum(
        "frwc,ijco->frwijo", padded, w_up, preferred_element_type=jnp.float32
    )
    phases_a = []
    for a in range(2):
        phases_b = []
        for b in range(2):
            acc = None
            for dr in range(3):
                ro = (a + dr + 1) // 2
                for dc in range(3):
                    co = (b + dc + 1) // 2
                    term = taps[:, ro : ro + nrows, co : co + ncols, dr, dc, :]
                    acc = term if acc is None else acc + term
            phases_b.append(acc)
        phases_a.append(jnp.stack(phases_b, axis=3))
    result = jnp.stack(phases_a, axis=2)
    return result.astype(jnp.bfloat16).reshape(nf, 2 * nrows, 2 * ncols * outs)


def layer(
    frames, norm_attn, w_query, w_key, w_value, w_out, cache_one, norm_conv, conv_weight, w_up
):
    nframes, nrows, ncols, chans = frames.shape
    scale = chans ** (-0.5)

    cache_haloed = padded_2(cache_one, ((ROWS, 1),), 2)
    cache_part = conv_rows(cache_haloed, conv_weight[:2])

    flat = frames.reshape(nframes, nrows * ncols, chans)
    normed = rms_gain(flat.astype(jnp.float32), norm_attn).astype(jnp.bfloat16)
    queries = project(normed, w_query)
    size = lax.axis_size(ROWS)
    chip_bits = [1 << k for k in range(1, size.bit_length() - 1)]
    low, high = chip_bits[:1], chip_bits[1:]
    half = normed.shape[1] // 2
    first, second = normed[:, :half], normed[:, half:]
    first_in = exchange(first, high, size)
    second_in = exchange(second, low, size)
    gathered = jnp.concatenate([first, second] + first_in + second_in, axis=1)
    first_out = exchange(jnp.concatenate([first] + first_in, axis=1), low, size)
    second_out = exchange(jnp.concatenate([second] + second_in, axis=1), high, size)
    mine = [gathered] + first_out + second_out
    pieces = mine + [exchange(piece, [1], size)[0] for piece in mine]
    q_keyed = jnp.einsum("fqc,dc->fqd", queries, w_key, preferred_element_type=jnp.float32)
    q_pair = split_pair(q_keyed, axis=1)
    count = queries.shape[1]
    scores = []
    for piece in pieces:
        both = jnp.einsum("fqc,fkc->fqk", q_pair, piece, preferred_element_type=jnp.float32)
        scores.append((both[:, :count] + both[:, count:]) * scale)
    top = jnp.max(jnp.stack([jnp.max(s, axis=-1) for s in scores], axis=-1), axis=-1)[..., None]
    expos = [jnp.exp(s - top) for s in scores]
    denom = sum(jnp.sum(e, axis=-1, keepdims=True) for e in expos)
    mixed_in = sum(
        jnp.einsum("fqk,fkc->fqc", e.astype(jnp.bfloat16), p, preferred_element_type=jnp.float32)
        for e, p in zip(expos, pieces)
    )
    both = jnp.einsum(
        "fqc,cd->fqd", split_pair(mixed_in, axis=1), w_value, preferred_element_type=jnp.float32
    )
    numer = both[:, :count] + both[:, count:]
    attended = (numer / denom).astype(jnp.bfloat16)
    mixed = (
        flat.astype(jnp.float32)
        + jnp.einsum("fqc,cd->fqd", attended, w_out, preferred_element_type=jnp.float32)
    ).astype(jnp.bfloat16)
    activ = (
        jax.nn.silu(rms_gain(mixed.astype(jnp.float32), norm_conv))
        .astype(jnp.bfloat16)
        .reshape(nframes, nrows, ncols, chans)
    )
    activ_haloed = padded_2(activ, ((ROWS, 1),), 2)
    extended = cache_part + conv_rows(activ_haloed, conv_weight[2:])
    where = lax.axis_index(ROWS)
    line = jnp.arange(nrows + 2)
    inside = ((line > 0) | (where > 0)) & ((line < nrows + 1) | (where < size - 1))
    extended = jnp.where(inside[None, :, None, None], extended, 0.0).astype(jnp.bfloat16)
    return upsample_conv(extended, w_up)


def solution(mesh):
    clips, rows = mesh.devices.shape
    mesh = jax.sharding.Mesh(mesh.devices.reshape(clips, rows // 2, 2), ("clips",) + ROWS)
    placed = (
        P("clips", ROWS, None, None),
        P(),
        P(),
        P(),
        P(),
        P(),
        P("clips", ROWS, None, None),
        P(),
        P(),
        P(),
    )
    return jax.shard_map(
        layer, mesh=mesh, in_specs=placed, out_specs=P("clips", ROWS, None), check_vma=False
    )
```

```python
import jax
import jax.numpy as jnp
from jax import lax
from jax.sharding import PartitionSpec as P

EPS = 1e-06


ROWS = ("chip", "core")


def padded_2(array, sides, width):
    for axis, dim in sides:
        size = lax.axis_size(axis)
        even = (lax.axis_index(axis) % 2) == 0
        first = lax.slice_in_dim(array, 0, width, axis=dim)
        last = lax.slice_in_dim(array, array.shape[dim] - width, array.shape[dim], axis=dim)
        on_chip = lax.ppermute(
            jnp.where(even, last, first), axis, [(i, i ^ 1) for i in range(size)]
        )
        pairs = [(i, i + 1) for i in range(1, size - 1, 2)]
        across = lax.ppermute(
            jnp.where(even, first, last), axis, pairs + [(j, i) for i, j in pairs]
        )
        before = jnp.where(even, across, on_chip)
        after = jnp.where(even, on_chip, across)
        array = jnp.concatenate([before, array, after], axis=dim)
    return array


def rms_gain(values, gain):
    return values * lax.rsqrt(jnp.mean(values * values, axis=-1, keepdims=True) + EPS) * gain


def project(inputs, weight):
    return jnp.einsum("fqc,cd->fqd", inputs, weight, preferred_element_type=jnp.float32).astype(
        jnp.bfloat16
    )


def exchange(values, bits, size):
    masks = [0]
    for bit in bits:
        masks = masks + [mask | bit for mask in masks]
    return [
        lax.ppermute(values, ROWS, [(i, i ^ mask) for i in range(size)]) for mask in masks[1:]
    ]


def split_pair(values, axis):
    high = values.astype(jnp.bfloat16)
    low = (values - high.astype(jnp.float32)).astype(jnp.bfloat16)
    return jnp.concatenate([high, low], axis=axis)


def conv_rows(haloed, weight):
    total = None
    for tstep in range(weight.shape[0]):
        part = lax.conv_general_dilated(
            haloed[tstep : tstep + 1],
            weight[tstep],
            window_strides=(1, 1),
            padding=((0, 0), (1, 1)),
            dimension_numbers=("NHWC", "HWIO", "NHWC"),
            preferred_element_type=jnp.float32,
        )
        total = part if total is None else total + part
    return total


def upsample_conv(extended, w_up):
    nf, rp, ncols, chans = extended.shape
    nrows = rp - 2
    outs = w_up.shape[-1]
    padded = jnp.pad(extended, ((0, 0), (0, 0), (1, 1), (0, 0)))
    taps = jnp.einsum(
        "frwc,ijco->frwijo", padded, w_up, preferred_element_type=jnp.float32
    )
    phases_a = []
    for a in range(2):
        phases_b = []
        for b in range(2):
            acc = None
            for dr in range(3):
                ro = (a + dr + 1) // 2
                for dc in range(3):
                    co = (b + dc + 1) // 2
                    term = taps[:, ro : ro + nrows, co : co + ncols, dr, dc, :]
                    acc = term if acc is None else acc + term
            phases_b.append(acc)
        phases_a.append(jnp.stack(phases_b, axis=3))
    result = jnp.stack(phases_a, axis=2)
    return result.astype(jnp.bfloat16).reshape(nf, 2 * nrows, 2 * ncols * outs)


def body(
    frames, norm_attn, w_query, w_key, w_value, w_out, cache_one, norm_conv, conv_weight, w_up
):
    nframes, nrows, ncols, chans = frames.shape
    scale = chans ** (-0.5)

    cache_haloed = padded_2(cache_one, ((ROWS, 1),), 1)
    cache_part = conv_rows(cache_haloed, conv_weight[:2])

    flat = frames.reshape(nframes, nrows * ncols, chans)
    normed = rms_gain(flat.astype(jnp.float32), norm_attn).astype(jnp.bfloat16)
    queries = project(normed, w_query)
    size = lax.axis_size(ROWS)
    chip_bits = [1 << k for k in range(1, size.bit_length() - 1)]
    low, high = chip_bits[:1], chip_bits[1:]
    half = normed.shape[1] // 2
    first, second = normed[:, :half], normed[:, half:]
    first_in = exchange(first, high, size)
    second_in = exchange(second, low, size)
    gathered = jnp.concatenate([first, second] + first_in + second_in, axis=1)
    first_out = exchange(jnp.concatenate([first] + first_in, axis=1), low, size)
    second_out = exchange(jnp.concatenate([second] + second_in, axis=1), high, size)
    mine = [gathered] + first_out + second_out
    pieces = mine + [exchange(piece, [1], size)[0] for piece in mine]
    q_keyed = jnp.einsum("fqc,dc->fqd", queries, w_key, preferred_element_type=jnp.float32)
    q_pair = split_pair(q_keyed, axis=1)
    count = queries.shape[1]
    scores = []
    for piece in pieces:
        both = jnp.einsum("fqc,fkc->fqk", q_pair, piece, preferred_element_type=jnp.float32)
        scores.append((both[:, :count] + both[:, count:]) * scale)
    top = jnp.max(jnp.stack([jnp.max(s, axis=-1) for s in scores], axis=-1), axis=-1)[..., None]
    expos = [jnp.exp(s - top) for s in scores]
    denom = sum(jnp.sum(e, axis=-1, keepdims=True) for e in expos)
    mixed_in = sum(
        jnp.einsum("fqk,fkc->fqc", e.astype(jnp.bfloat16), p, preferred_element_type=jnp.float32)
        for e, p in zip(expos, pieces)
    )
    both = jnp.einsum(
        "fqc,cd->fqd", split_pair(mixed_in, axis=1), w_value, preferred_element_type=jnp.float32
    )
    numer = both[:, :count] + both[:, count:]
    attended = (numer / denom).astype(jnp.bfloat16)
    mixed = (
        flat.astype(jnp.float32)
        + jnp.einsum("fqc,cd->fqd", attended, w_out, preferred_element_type=jnp.float32)
    ).astype(jnp.bfloat16)
    activ = (
        jax.nn.silu(rms_gain(mixed.astype(jnp.float32), norm_conv))
        .astype(jnp.bfloat16)
        .reshape(nframes, nrows, ncols, chans)
    )
    activ_haloed = padded_2(activ, ((ROWS, 1),), 1)
    conv_out = (cache_part + conv_rows(activ_haloed, conv_weight[2:])).astype(jnp.bfloat16)
    extended = padded_2(conv_out, ((ROWS, 1),), 1)
    return upsample_conv(extended, w_up)


def solution(mesh):
    clips, rows = mesh.devices.shape
    mesh = jax.sharding.Mesh(mesh.devices.reshape(clips, rows // 2, 2), ("clips",) + ROWS)
    placed = (
        P("clips", ROWS, None, None),
        P(),
        P(),
        P(),
        P(),
        P(),
        P("clips", ROWS, None, None),
        P(),
        P(),
        P(),
    )
    return jax.shard_map(
        body, mesh=mesh, in_specs=placed, out_specs=P("clips", ROWS, None), check_vma=False
    )
```

```python
import jax
import jax.numpy as jnp
from jax import lax
from jax.sharding import PartitionSpec as P

EPS = 1e-06


ROWS = ("chip", "core")


def padded_2(array, sides, width):
    for axis, dim in sides:
        size = lax.axis_size(axis)
        even = (lax.axis_index(axis) % 2) == 0
        first = lax.slice_in_dim(array, 0, width, axis=dim)
        last = lax.slice_in_dim(array, array.shape[dim] - width, array.shape[dim], axis=dim)
        on_chip = lax.ppermute(
            jnp.where(even, last, first), axis, [(i, i ^ 1) for i in range(size)]
        )
        pairs = [(i, i + 1) for i in range(1, size - 1, 2)]
        across = lax.ppermute(
            jnp.where(even, first, last), axis, pairs + [(j, i) for i, j in pairs]
        )
        before = jnp.where(even, across, on_chip)
        after = jnp.where(even, on_chip, across)
        array = jnp.concatenate([before, array, after], axis=dim)
    return array


def halo_pair(array, axis, width):
    haloed = padded_2(array, ((axis, 1),), width)
    return haloed[:, :width], haloed[:, -width:]


def rms_gain(values, gain):
    return values * lax.rsqrt(jnp.mean(values * values, axis=-1, keepdims=True) + EPS) * gain


def project(inputs, weight):
    return jnp.einsum("fqc,cd->fqd", inputs, weight, preferred_element_type=jnp.float32).astype(
        jnp.bfloat16
    )


def exchange(values, bits, size):
    masks = [0]
    for bit in bits:
        masks = masks + [mask | bit for mask in masks]
    return [
        lax.ppermute(values, ROWS, [(i, i ^ mask) for i in range(size)]) for mask in masks[1:]
    ]


def tap_row(rows, weight):
    return lax.conv_general_dilated(
        rows,
        weight[None],
        window_strides=(1, 1),
        padding=((0, 0), (1, 1)),
        dimension_numbers=("NHWC", "HWIO", "NHWC"),
        preferred_element_type=jnp.float32,
    )


def split_pair(values, axis):
    high = values.astype(jnp.bfloat16)
    low = (values - high.astype(jnp.float32)).astype(jnp.bfloat16)
    return jnp.concatenate([high, low], axis=axis)


def conv_rows(haloed, weight):
    total = None
    for tstep in range(weight.shape[0]):
        part = lax.conv_general_dilated(
            haloed[tstep : tstep + 1],
            weight[tstep],
            window_strides=(1, 1),
            padding=((0, 0), (1, 1)),
            dimension_numbers=("NHWC", "HWIO", "NHWC"),
            preferred_element_type=jnp.float32,
        )
        total = part if total is None else total + part
    return total


def upsample_conv(before, middle, after, w_up):
    nf, nrows, ncols, chans = middle.shape
    outs = w_up.shape[-1]

    def taps_of(rows):
        padded = jnp.pad(rows, ((0, 0), (0, 0), (1, 1), (0, 0)))
        return jnp.einsum("frwc,ijco->frwijo", padded, w_up, preferred_element_type=jnp.float32)

    mid, top, bottom = taps_of(middle), taps_of(before), taps_of(after)
    shifted = {
        0: lambda dr, co: jnp.concatenate(
            [top[:, :, co : co + ncols, dr], mid[:, : nrows - 1, co : co + ncols, dr]], axis=1
        ),
        1: lambda dr, co: mid[:, :, co : co + ncols, dr],
        2: lambda dr, co: jnp.concatenate(
            [mid[:, 1:, co : co + ncols, dr], bottom[:, :, co : co + ncols, dr]], axis=1
        ),
    }
    phases_a = []
    for a in range(2):
        phases_b = []
        for b in range(2):
            acc = None
            for dr in range(3):
                ro = (a + dr + 1) // 2
                for dc in range(3):
                    co = (b + dc + 1) // 2
                    term = shifted[ro](dr, co)[:, :, :, dc, :]
                    acc = term if acc is None else acc + term
            phases_b.append(acc)
        phases_a.append(jnp.stack(phases_b, axis=3))
    result = jnp.stack(phases_a, axis=2)
    return result.astype(jnp.bfloat16).reshape(nf, 2 * nrows, 2 * ncols * outs)


def body(
    frames, norm_attn, w_query, w_key, w_value, w_out, cache_one, norm_conv, conv_weight, w_up
):
    nframes, nrows, ncols, chans = frames.shape
    scale = chans ** (-0.5)

    cache_haloed = padded_2(cache_one, ((ROWS, 1),), 1)
    cache_part = conv_rows(cache_haloed, conv_weight[:2])

    flat = frames.reshape(nframes, nrows * ncols, chans)
    normed = rms_gain(flat.astype(jnp.float32), norm_attn).astype(jnp.bfloat16)
    queries = project(normed, w_query)
    size = lax.axis_size(ROWS)
    chip_bits = [1 << k for k in range(1, size.bit_length() - 1)]
    low, high = chip_bits[:1], chip_bits[1:]
    half = normed.shape[1] // 2
    first, second = normed[:, :half], normed[:, half:]
    first_in = exchange(first, high, size)
    second_in = exchange(second, low, size)
    gathered = jnp.concatenate([first, second] + first_in + second_in, axis=1)
    first_out = exchange(jnp.concatenate([first] + first_in, axis=1), low, size)
    second_out = exchange(jnp.concatenate([second] + second_in, axis=1), high, size)
    mine = [gathered] + first_out + second_out
    pieces = mine + [exchange(piece, [1], size)[0] for piece in mine]
    q_keyed = jnp.einsum("fqc,dc->fqd", queries, w_key, preferred_element_type=jnp.float32)
    q_pair = split_pair(q_keyed, axis=1)
    count = queries.shape[1]
    scores = []
    for piece in pieces:
        both = jnp.einsum("fqc,fkc->fqk", q_pair, piece, preferred_element_type=jnp.float32)
        scores.append((both[:, :count] + both[:, count:]) * scale)
    top = jnp.max(jnp.stack([jnp.max(s, axis=-1) for s in scores], axis=-1), axis=-1)[..., None]
    expos = [jnp.exp(s - top) for s in scores]
    denom = sum(jnp.sum(e, axis=-1, keepdims=True) for e in expos)
    mixed_in = sum(
        jnp.einsum("fqk,fkc->fqc", e.astype(jnp.bfloat16), p, preferred_element_type=jnp.float32)
        for e, p in zip(expos, pieces)
    )
    both = jnp.einsum(
        "fqc,cd->fqd", split_pair(mixed_in, axis=1), w_value, preferred_element_type=jnp.float32
    )
    numer = both[:, :count] + both[:, count:]
    attended = (numer / denom).astype(jnp.bfloat16)
    mixed = (
        flat.astype(jnp.float32)
        + jnp.einsum("fqc,cd->fqd", attended, w_out, preferred_element_type=jnp.float32)
    ).astype(jnp.bfloat16)
    activ = (
        jax.nn.silu(rms_gain(mixed.astype(jnp.float32), norm_conv))
        .astype(jnp.bfloat16)
        .reshape(nframes, nrows, ncols, chans)
    )
    above, below = halo_pair(activ, ROWS, 1)
    weight = conv_weight[2]
    total = cache_part + tap_row(activ, weight[1])
    total = total + tap_row(jnp.concatenate([above, activ[:, :-1]], axis=1), weight[0])
    total = total + tap_row(jnp.concatenate([activ[:, 1:], below], axis=1), weight[2])
    conv_out = total.astype(jnp.bfloat16)
    before, after = halo_pair(conv_out, ROWS, 1)
    return upsample_conv(before, conv_out, after, w_up)


def solution(mesh):
    clips, rows = mesh.devices.shape
    mesh = jax.sharding.Mesh(mesh.devices.reshape(clips, rows // 2, 2), ("clips",) + ROWS)
    placed = (
        P("clips", ROWS, None, None),
        P(),
        P(),
        P(),
        P(),
        P(),
        P("clips", ROWS, None, None),
        P(),
        P(),
        P(),
    )
    return jax.shard_map(
        body, mesh=mesh, in_specs=placed, out_specs=P("clips", ROWS, None), check_vma=False
    )
```

```python
import jax
import jax.numpy as jnp
from jax import lax
from jax.sharding import PartitionSpec as P

EPS = 1e-06


ROWS = ("chip", "core")


def padded_2(array, sides, width):
    for axis, dim in sides:
        size = lax.axis_size(axis)
        even = (lax.axis_index(axis) % 2) == 0
        first = lax.slice_in_dim(array, 0, width, axis=dim)
        last = lax.slice_in_dim(array, array.shape[dim] - width, array.shape[dim], axis=dim)
        on_chip = lax.ppermute(
            jnp.where(even, last, first), axis, [(i, i ^ 1) for i in range(size)]
        )
        pairs = [(i, i + 1) for i in range(1, size - 1, 2)]
        across = lax.ppermute(
            jnp.where(even, first, last), axis, pairs + [(j, i) for i, j in pairs]
        )
        before = jnp.where(even, across, on_chip)
        after = jnp.where(even, on_chip, across)
        array = jnp.concatenate([before, array, after], axis=dim)
    return array


def rms_gain(values, gain):
    return values * lax.rsqrt(jnp.mean(values * values, axis=-1, keepdims=True) + EPS) * gain


def project(inputs, weight):
    return jnp.einsum("fqc,cd->fqd", inputs, weight, preferred_element_type=jnp.float32).astype(
        jnp.bfloat16
    )


def exchange(values, bits, size):
    masks = [0]
    for bit in bits:
        masks = masks + [mask | bit for mask in masks]
    return [
        lax.ppermute(values, ROWS, [(i, i ^ mask) for i in range(size)]) for mask in masks[1:]
    ]


def split_pair(values, axis):
    high = values.astype(jnp.bfloat16)
    low = (values - high.astype(jnp.float32)).astype(jnp.bfloat16)
    return jnp.concatenate([high, low], axis=axis)


def conv_rows(haloed, weight):
    total = None
    for tstep in range(weight.shape[0]):
        part = lax.conv_general_dilated(
            haloed[tstep : tstep + 1],
            weight[tstep],
            window_strides=(1, 1),
            padding=((0, 0), (1, 1)),
            dimension_numbers=("NHWC", "HWIO", "NHWC"),
            preferred_element_type=jnp.float32,
        )
        total = part if total is None else total + part
    return total


def upsample_conv(extended, w_up):
    nf, rp, ncols, chans = extended.shape
    nrows = rp - 2
    outs = w_up.shape[-1]
    padded = jnp.pad(extended, ((0, 0), (0, 0), (1, 1), (0, 0)))
    taps = jnp.einsum(
        "frwc,ijco->frwijo", padded, w_up, preferred_element_type=jnp.float32
    )
    phases_a = []
    for a in range(2):
        phases_b = []
        for b in range(2):
            acc = None
            for dr in range(3):
                ro = (a + dr + 1) // 2
                for dc in range(3):
                    co = (b + dc + 1) // 2
                    term = taps[:, ro : ro + nrows, co : co + ncols, dr, dc, :]
                    acc = term if acc is None else acc + term
            phases_b.append(acc)
        phases_a.append(jnp.stack(phases_b, axis=3))
    result = jnp.stack(phases_a, axis=2)
    return result.astype(jnp.bfloat16).reshape(nf, 2 * nrows, 2 * ncols * outs)


def body(
    frames, norm_attn, w_query, w_key, w_value, w_out, cache_one, norm_conv, conv_weight, w_up
):
    nframes, nrows, ncols, chans = frames.shape
    scale = chans ** (-0.5)

    cache_haloed = padded_2(cache_one, ((ROWS, 1),), 2)
    cache_part = conv_rows(cache_haloed, conv_weight[:2])

    flat = frames.reshape(nframes, nrows * ncols, chans)
    normed = rms_gain(flat.astype(jnp.float32), norm_attn).astype(jnp.bfloat16)
    queries = project(normed, w_query)
    size = lax.axis_size(ROWS)
    chip_bits = [1 << k for k in range(1, size.bit_length() - 1)]
    low, high = chip_bits[:1], chip_bits[1:]
    half = normed.shape[1] // 2
    first, second = normed[:, :half], normed[:, half:]
    first_in = exchange(first, high, size)
    second_in = exchange(second, low, size)
    gathered = jnp.concatenate([first, second] + first_in + second_in, axis=1)
    first_out = exchange(jnp.concatenate([first] + first_in, axis=1), low, size)
    second_out = exchange(jnp.concatenate([second] + second_in, axis=1), high, size)
    mine = [gathered] + first_out + second_out
    pieces = mine + [exchange(piece, [1], size)[0] for piece in mine]
    q_keyed = jnp.einsum("fqc,dc->fqd", queries, w_key, preferred_element_type=jnp.float32)
    q_pair = split_pair(q_keyed, axis=1)
    count = queries.shape[1]
    scores = []
    for piece in pieces:
        both = jnp.einsum("fqc,fkc->fqk", q_pair, piece, preferred_element_type=jnp.float32)
        scores.append((both[:, :count] + both[:, count:]) * scale)
    top = jnp.max(jnp.stack([jnp.max(s, axis=-1) for s in scores], axis=-1), axis=-1)[..., None]
    expos = [jnp.exp(s - top) for s in scores]
    denom = sum(jnp.sum(e, axis=-1, keepdims=True) for e in expos)
    mixed_in = sum(
        jnp.einsum("fqk,fkc->fqc", e.astype(jnp.bfloat16), p, preferred_element_type=jnp.float32)
        for e, p in zip(expos, pieces)
    )
    both = jnp.einsum(
        "fqc,cd->fqd", split_pair(mixed_in, axis=1), w_value, preferred_element_type=jnp.float32
    )
    numer = both[:, :count] + both[:, count:]
    attended = (numer / denom).astype(jnp.bfloat16)
    mixed = (
        flat.astype(jnp.float32)
        + jnp.einsum("fqc,cd->fqd", attended, w_out, preferred_element_type=jnp.float32)
    ).astype(jnp.bfloat16)
    activ = (
        jax.nn.silu(rms_gain(mixed.astype(jnp.float32), norm_conv))
        .astype(jnp.bfloat16)
        .reshape(nframes, nrows, ncols, chans)
    )
    activ_haloed = padded_2(activ, ((ROWS, 1),), 2)
    extended = cache_part + conv_rows(activ_haloed, conv_weight[2:])
    where = lax.axis_index(ROWS)
    line = jnp.arange(nrows + 2)
    inside = ((line > 0) | (where > 0)) & ((line < nrows + 1) | (where < size - 1))
    extended = jnp.where(inside[None, :, None, None], extended, 0.0).astype(jnp.bfloat16)
    return upsample_conv(extended, w_up)


def solution(mesh):
    clips, rows = mesh.devices.shape
    mesh = jax.sharding.Mesh(mesh.devices.reshape(clips, rows // 2, 2), ("clips",) + ROWS)
    placed = (
        P("clips", ROWS, None, None),
        P(),
        P(),
        P(),
        P(),
        P(),
        P("clips", ROWS, None, None),
        P(),
        P(),
        P(),
    )
    return jax.shard_map(
        body, mesh=mesh, in_specs=placed, out_specs=P("clips", ROWS, None), check_vma=False
    )
```

```python
import jax
import jax.numpy as jnp
from jax import lax
from jax.sharding import PartitionSpec as P

EPS = 1e-06


ROWS = ("chip", "core")


def padded_2(array, sides, width):
    for axis, dim in sides:
        size = lax.axis_size(axis)
        even = (lax.axis_index(axis) % 2) == 0
        first = lax.slice_in_dim(array, 0, width, axis=dim)
        last = lax.slice_in_dim(array, array.shape[dim] - width, array.shape[dim], axis=dim)
        on_chip = lax.ppermute(
            jnp.where(even, last, first), axis, [(i, i ^ 1) for i in range(size)]
        )
        pairs = [(i, i + 1) for i in range(1, size - 1, 2)]
        across = lax.ppermute(
            jnp.where(even, first, last), axis, pairs + [(j, i) for i, j in pairs]
        )
        before = jnp.where(even, across, on_chip)
        after = jnp.where(even, on_chip, across)
        array = jnp.concatenate([before, array, after], axis=dim)
    return array


def rms_gain(values, gain):
    return values * lax.rsqrt(jnp.mean(values * values, axis=-1, keepdims=True) + EPS) * gain


def project(inputs, weight):
    return jnp.einsum("fqc,cd->fqd", inputs, weight, preferred_element_type=jnp.float32).astype(
        jnp.bfloat16
    )


def exchange(values, bits, size):
    masks = [0]
    for bit in bits:
        masks = masks + [mask | bit for mask in masks]
    return [
        lax.ppermute(values, ROWS, [(i, i ^ mask) for i in range(size)]) for mask in masks[1:]
    ]


def split_pair(values, axis):
    high = values.astype(jnp.bfloat16)
    low = (values - high.astype(jnp.float32)).astype(jnp.bfloat16)
    return jnp.concatenate([high, low], axis=axis)


def conv_rows(haloed, weight):
    total = None
    for tstep in range(weight.shape[0]):
        part = lax.conv_general_dilated(
            haloed[tstep : tstep + 1],
            weight[tstep],
            window_strides=(1, 1),
            padding=((0, 0), (1, 1)),
            dimension_numbers=("NHWC", "HWIO", "NHWC"),
            preferred_element_type=jnp.float32,
        )
        total = part if total is None else total + part
    return total


def upsample_conv(extended, w_up):
    nf, rp, ncols, chans = extended.shape
    nrows = rp - 2
    outs = w_up.shape[-1]
    padded = jnp.pad(extended, ((0, 0), (0, 0), (1, 1), (0, 0)))
    taps = jnp.einsum(
        "frwc,ijco->frwijo", padded, w_up, preferred_element_type=jnp.float32
    )
    phases_a = []
    for a in range(2):
        phases_b = []
        for b in range(2):
            acc = None
            for dr in range(3):
                ro = (a + dr + 1) // 2
                for dc in range(3):
                    co = (b + dc + 1) // 2
                    term = taps[:, ro : ro + nrows, co : co + ncols, dr, dc, :]
                    acc = term if acc is None else acc + term
            phases_b.append(acc)
        phases_a.append(jnp.stack(phases_b, axis=3))
    result = jnp.stack(phases_a, axis=2)
    return result.astype(jnp.bfloat16).reshape(nf, 2 * nrows, 2 * ncols * outs)


def body(
    frames, norm_attn, w_query, w_key, w_value, w_out, cache_one, norm_conv, conv_weight, w_up
):
    nframes, nrows, ncols, chans = frames.shape
    scale = chans ** (-0.5)

    cache_haloed = padded_2(cache_one, ((ROWS, 1),), 1)
    cache_part = conv_rows(cache_haloed, conv_weight[:2])

    flat = frames.reshape(nframes, nrows * ncols, chans)
    normed = rms_gain(flat.astype(jnp.float32), norm_attn).astype(jnp.bfloat16)
    queries = project(normed, w_query)
    size = lax.axis_size(ROWS)
    chip_bits = [1 << k for k in range(1, size.bit_length() - 1)]
    low, high = chip_bits[:1], chip_bits[1:]
    half = normed.shape[1] // 2
    first, second = normed[:, :half], normed[:, half:]
    first_in = exchange(first, high, size)
    second_in = exchange(second, low, size)
    gathered = jnp.concatenate([first, second] + first_in + second_in, axis=1)
    first_out = exchange(jnp.concatenate([first] + first_in, axis=1), low, size)
    second_out = exchange(jnp.concatenate([second] + second_in, axis=1), high, size)
    mine = [gathered] + first_out + second_out
    pieces = mine + [exchange(piece, [1], size)[0] for piece in mine]
    q_keyed = jnp.einsum("fqc,dc->fqd", queries, w_key, preferred_element_type=jnp.float32)
    q_pair = split_pair(q_keyed, axis=1)
    count = queries.shape[1]
    groups = [[mine[0], pieces[len(mine)]], mine[1:], pieces[len(mine) + 1 :]]
    top = denom = mixed_in = None
    for group in groups:
        scores = []
        for piece in group:
            both = jnp.einsum("fqc,fkc->fqk", q_pair, piece, preferred_element_type=jnp.float32)
            scores.append((both[:, :count] + both[:, count:]) * scale)
        peak = jnp.max(jnp.stack([jnp.max(s, axis=-1) for s in scores], axis=-1), axis=-1)
        new_top = peak[..., None] if top is None else jnp.maximum(top, peak[..., None])
        expos = [jnp.exp(s - new_top) for s in scores]
        part_denom = sum(jnp.sum(e, axis=-1, keepdims=True) for e in expos)
        part_mixed = sum(
            jnp.einsum(
                "fqk,fkc->fqc", e.astype(jnp.bfloat16), p, preferred_element_type=jnp.float32
            )
            for e, p in zip(expos, group)
        )
        if top is None:
            denom, mixed_in = part_denom, part_mixed
        else:
            shrink = jnp.exp(top - new_top)
            denom = denom * shrink + part_denom
            mixed_in = mixed_in * shrink + part_mixed
        top = new_top
    both = jnp.einsum(
        "fqc,cd->fqd", split_pair(mixed_in, axis=1), w_value, preferred_element_type=jnp.float32
    )
    numer = both[:, :count] + both[:, count:]
    attended = (numer / denom).astype(jnp.bfloat16)
    mixed = (
        flat.astype(jnp.float32)
        + jnp.einsum("fqc,cd->fqd", attended, w_out, preferred_element_type=jnp.float32)
    ).astype(jnp.bfloat16)
    activ = (
        jax.nn.silu(rms_gain(mixed.astype(jnp.float32), norm_conv))
        .astype(jnp.bfloat16)
        .reshape(nframes, nrows, ncols, chans)
    )
    activ_haloed = padded_2(activ, ((ROWS, 1),), 1)
    conv_out = (cache_part + conv_rows(activ_haloed, conv_weight[2:])).astype(jnp.bfloat16)
    extended = padded_2(conv_out, ((ROWS, 1),), 1)
    return upsample_conv(extended, w_up)


def solution(mesh):
    clips, rows = mesh.devices.shape
    mesh = jax.sharding.Mesh(mesh.devices.reshape(clips, rows // 2, 2), ("clips",) + ROWS)
    placed = (
        P("clips", ROWS, None, None),
        P(),
        P(),
        P(),
        P(),
        P(),
        P("clips", ROWS, None, None),
        P(),
        P(),
        P(),
    )
    return jax.shard_map(
        body, mesh=mesh, in_specs=placed, out_specs=P("clips", ROWS, None), check_vma=False
    )
```

```python
import jax
import jax.numpy as jnp
from jax import lax
from jax.sharding import PartitionSpec as P


EPS = 1e-06


ROWS = ("chip", "core")


def padded_2(array, sides, width):
    for axis, dim in sides:
        size = lax.axis_size(axis)
        even = (lax.axis_index(axis) % 2) == 0
        first = lax.slice_in_dim(array, 0, width, axis=dim)
        last = lax.slice_in_dim(array, array.shape[dim] - width, array.shape[dim], axis=dim)
        on_chip = lax.ppermute(
            jnp.where(even, last, first), axis, [(i, i ^ 1) for i in range(size)]
        )
        pairs = [(i, i + 1) for i in range(1, size - 1, 2)]
        across = lax.ppermute(
            jnp.where(even, first, last), axis, pairs + [(j, i) for i, j in pairs]
        )
        before = jnp.where(even, across, on_chip)
        after = jnp.where(even, on_chip, across)
        array = jnp.concatenate([before, array, after], axis=dim)
    return array


def rms_gain(values, gain):
    return values * lax.rsqrt(jnp.mean(values * values, axis=-1, keepdims=True) + EPS) * gain


def project(inputs, weight):
    return jnp.einsum("fqc,cd->fqd", inputs, weight, preferred_element_type=jnp.float32).astype(
        jnp.bfloat16
    )


def exchange(values, bits, size):
    masks = [0]
    for bit in bits:
        masks = masks + [mask | bit for mask in masks]
    return [
        lax.ppermute(values, ROWS, [(i, i ^ mask) for i in range(size)]) for mask in masks[1:]
    ]


def split_pair(values, axis):
    high = values.astype(jnp.bfloat16)
    low = (values - high.astype(jnp.float32)).astype(jnp.bfloat16)
    return jnp.concatenate([high, low], axis=axis)


def conv_rows(haloed, weight):
    total = None
    for tstep in range(weight.shape[0]):
        part = lax.conv_general_dilated(
            haloed[tstep : tstep + 1],
            weight[tstep],
            window_strides=(1, 1),
            padding=((0, 0), (1, 1)),
            dimension_numbers=("NHWC", "HWIO", "NHWC"),
            preferred_element_type=jnp.float32,
        )
        total = part if total is None else total + part
    return total


def upsample_conv(extended, w_up):
    nf, rp, ncols, _ = extended.shape
    nrows = rp - 2
    outs = w_up.shape[-1]
    padded = jnp.pad(extended, ((0, 0), (0, 0), (1, 1), (0, 0)))
    taps = jnp.einsum(
        "frwc,ijco->frwijo", padded, w_up, preferred_element_type=jnp.float32
    )
    phases_a = []
    for a in range(2):
        phases_b = []
        for b in range(2):
            acc = None
            for dr in range(3):
                ro = (a + dr + 1) // 2
                for dc in range(3):
                    co = (b + dc + 1) // 2
                    term = taps[:, ro : ro + nrows, co : co + ncols, dr, dc, :]
                    acc = term if acc is None else acc + term
            phases_b.append(acc)
        phases_a.append(jnp.stack(phases_b, axis=3))
    result = jnp.stack(phases_a, axis=2)
    return result.astype(jnp.bfloat16).reshape(nf, 2 * nrows, 2 * ncols * outs)


def layer(
    frames, norm_attn, w_query, w_key, w_value, w_out, cache_one, norm_conv, conv_weight, w_up
):
    nframes, nrows, ncols, chans = frames.shape
    scale = chans ** (-0.5)

    cache_haloed = padded_2(cache_one, ((ROWS, 1),), 1)
    cache_part = conv_rows(cache_haloed, conv_weight[:2])

    flat = frames.reshape(nframes, nrows * ncols, chans)
    normed = rms_gain(flat.astype(jnp.float32), norm_attn).astype(jnp.bfloat16)
    queries = project(normed, w_query)
    size = lax.axis_size(ROWS)
    chip_bits = [1 << k for k in range(1, size.bit_length() - 1)]
    low, high = chip_bits[:1], chip_bits[1:]
    half = normed.shape[1] // 2
    first, second = normed[:, :half], normed[:, half:]
    first_in = exchange(first, high, size)
    second_in = exchange(second, low, size)
    gathered = jnp.concatenate([first, second] + first_in + second_in, axis=1)
    first_out = exchange(jnp.concatenate([first] + first_in, axis=1), low, size)
    second_out = exchange(jnp.concatenate([second] + second_in, axis=1), high, size)
    mine = [gathered] + first_out + second_out
    mirrors = exchange(gathered, [1], size)
    mirrors = mirrors + [exchange(piece, [1], size)[0] for piece in mine[1:]]
    pieces = mine + mirrors
    q_keyed = jnp.einsum("fqc,dc->fqd", queries, w_key, preferred_element_type=jnp.float32)
    q_pair = split_pair(q_keyed, axis=1)
    count = queries.shape[1]
    groups = [[mine[0], pieces[len(mine)]], mine[1:], pieces[len(mine) + 1 :]]
    top = denom = mixed_in = None
    for group in groups:
        scores = []
        for piece in group:
            both = jnp.einsum("fqc,fkc->fqk", q_pair, piece, preferred_element_type=jnp.float32)
            scores.append((both[:, :count] + both[:, count:]) * scale)
        peak = jnp.max(jnp.stack([jnp.max(s, axis=-1) for s in scores], axis=-1), axis=-1)
        new_top = peak[..., None] if top is None else jnp.maximum(top, peak[..., None])
        expos = [jnp.exp(s - new_top) for s in scores]
        part_denom = sum(jnp.sum(e, axis=-1, keepdims=True) for e in expos)
        part_mixed = sum(
            jnp.einsum(
                "fqk,fkc->fqc", e.astype(jnp.bfloat16), p, preferred_element_type=jnp.float32
            )
            for e, p in zip(expos, group)
        )
        if top is None:
            denom, mixed_in = part_denom, part_mixed
        else:
            shrink = jnp.exp(top - new_top)
            denom = denom * shrink + part_denom
            mixed_in = mixed_in * shrink + part_mixed
        top, denom, mixed_in = lax.optimization_barrier((new_top, denom, mixed_in))
    both = jnp.einsum(
        "fqc,cd->fqd", split_pair(mixed_in, axis=1), w_value, preferred_element_type=jnp.float32
    )
    numer = both[:, :count] + both[:, count:]
    attended = (numer / denom).astype(jnp.bfloat16)
    mixed = (
        flat.astype(jnp.float32)
        + jnp.einsum("fqc,cd->fqd", attended, w_out, preferred_element_type=jnp.float32)
    ).astype(jnp.bfloat16)
    activ = (
        jax.nn.silu(rms_gain(mixed.astype(jnp.float32), norm_conv))
        .astype(jnp.bfloat16)
        .reshape(nframes, nrows, ncols, chans)
    )
    activ_haloed = padded_2(activ, ((ROWS, 1),), 1)
    conv_out = (cache_part + conv_rows(activ_haloed, conv_weight[2:])).astype(jnp.bfloat16)
    extended = padded_2(conv_out, ((ROWS, 1),), 1)
    return upsample_conv(extended, w_up)


def solution(mesh):
    clips, rows = mesh.devices.shape
    mesh = jax.sharding.Mesh(mesh.devices.reshape(clips, rows // 2, 2), ("clips",) + ROWS)
    placed = (
        P("clips", ROWS, None, None),
        P(),
        P(),
        P(),
        P(),
        P(),
        P("clips", ROWS, None, None),
        P(),
        P(),
        P(),
    )
    return jax.shard_map(
        layer, mesh=mesh, in_specs=placed, out_specs=P("clips", ROWS, None), check_vma=False
    )
```

```python
import jax
import jax.numpy as jnp
from jax import lax
from jax.sharding import PartitionSpec as P


EPS = 1e-06


ROWS = ("chip", "core")


def padded_2(array, sides, width):
    for axis, dim in sides:
        size = lax.axis_size(axis)
        even = (lax.axis_index(axis) % 2) == 0
        first = lax.slice_in_dim(array, 0, width, axis=dim)
        last = lax.slice_in_dim(array, array.shape[dim] - width, array.shape[dim], axis=dim)
        on_chip = lax.ppermute(
            jnp.where(even, last, first), axis, [(i, i ^ 1) for i in range(size)]
        )
        pairs = [(i, i + 1) for i in range(1, size - 1, 2)]
        across = lax.ppermute(
            jnp.where(even, first, last), axis, pairs + [(j, i) for i, j in pairs]
        )
        before = jnp.where(even, across, on_chip)
        after = jnp.where(even, on_chip, across)
        array = jnp.concatenate([before, array, after], axis=dim)
    return array


def rms_gain(values, gain):
    return values * lax.rsqrt(jnp.mean(values * values, axis=-1, keepdims=True) + EPS) * gain


def project(inputs, weight):
    return jnp.einsum("fqc,cd->fqd", inputs, weight, preferred_element_type=jnp.float32).astype(
        jnp.bfloat16
    )


def exchange(values, bits, size):
    masks = [0]
    for bit in bits:
        masks = masks + [mask | bit for mask in masks]
    return [
        lax.ppermute(values, ROWS, [(i, i ^ mask) for i in range(size)]) for mask in masks[1:]
    ]


def tap_row(rows, weight):
    return lax.conv_general_dilated(
        rows,
        weight[None],
        window_strides=(1, 1),
        padding=((0, 0), (1, 1)),
        dimension_numbers=("NHWC", "HWIO", "NHWC"),
        preferred_element_type=jnp.float32,
    )


def split_pair(values, axis):
    high = values.astype(jnp.bfloat16)
    low = (values - high.astype(jnp.float32)).astype(jnp.bfloat16)
    return jnp.concatenate([high, low], axis=axis)


def conv_rows(haloed, weight):
    total = None
    for tstep in range(weight.shape[0]):
        part = lax.conv_general_dilated(
            haloed[tstep : tstep + 1],
            weight[tstep],
            window_strides=(1, 1),
            padding=((0, 0), (1, 1)),
            dimension_numbers=("NHWC", "HWIO", "NHWC"),
            preferred_element_type=jnp.float32,
        )
        total = part if total is None else total + part
    return total


def upsample_conv(extended, w_up):
    nf, rp, ncols, _ = extended.shape
    nrows = rp - 2
    outs = w_up.shape[-1]
    padded = jnp.pad(extended, ((0, 0), (0, 0), (1, 1), (0, 0)))
    taps = jnp.einsum(
        "frwc,ijco->frwijo", padded, w_up, preferred_element_type=jnp.float32
    )
    phases_a = []
    for a in range(2):
        phases_b = []
        for b in range(2):
            acc = None
            for dr in range(3):
                ro = (a + dr + 1) // 2
                for dc in range(3):
                    co = (b + dc + 1) // 2
                    term = taps[:, ro : ro + nrows, co : co + ncols, dr, dc, :]
                    acc = term if acc is None else acc + term
            phases_b.append(acc)
        phase = jnp.concatenate(phases_b, axis=-1).astype(jnp.bfloat16)
        phases_a.append(phase.reshape(nf, nrows, 2 * ncols * outs))
    result = jnp.stack(phases_a, axis=2)
    return result.reshape(nf, 2 * nrows, 2 * ncols * outs)


def layer(
    frames, norm_attn, w_query, w_key, w_value, w_out, cache_one, norm_conv, conv_weight, w_up
):
    nframes, nrows, ncols, chans = frames.shape
    scale = chans ** (-0.5)

    cache_haloed = padded_2(cache_one, ((ROWS, 1),), 1)
    cache_part = conv_rows(cache_haloed, conv_weight[:2])

    flat = frames.reshape(nframes, nrows * ncols, chans)
    normed = rms_gain(flat.astype(jnp.float32), norm_attn).astype(jnp.bfloat16)
    queries = project(normed, w_query)
    size = lax.axis_size(ROWS)
    chip_bits = [1 << k for k in range(1, size.bit_length() - 1)]
    low, high = chip_bits[:1], chip_bits[1:]
    half = normed.shape[1] // 2
    first, second = normed[:, :half], normed[:, half:]
    first_in = exchange(first, high, size)
    second_in = exchange(second, low, size)
    gathered = jnp.concatenate([first, second] + first_in + second_in, axis=1)
    first_out = exchange(jnp.concatenate([first] + first_in, axis=1), low, size)
    second_out = exchange(jnp.concatenate([second] + second_in, axis=1), high, size)
    mine = [gathered] + first_out + second_out
    mirrors = exchange(gathered, [1], size)
    mirrors = mirrors + [exchange(piece, [1], size)[0] for piece in mine[1:]]
    pieces = mine + mirrors
    q_keyed = jnp.einsum("fqc,dc->fqd", queries, w_key, preferred_element_type=jnp.float32)
    q_pair = split_pair(q_keyed, axis=1)
    count = queries.shape[1]
    groups = [[mine[0], pieces[len(mine)]], mine[1:], pieces[len(mine) + 1 :]]
    top = denom = mixed_in = None
    for group in groups:
        scores = []
        for piece in group:
            both = jnp.einsum("fqc,fkc->fqk", q_pair, piece, preferred_element_type=jnp.float32)
            scores.append((both[:, :count] + both[:, count:]) * scale)
        peak = jnp.max(jnp.stack([jnp.max(s, axis=-1) for s in scores], axis=-1), axis=-1)
        new_top = peak[..., None] if top is None else jnp.maximum(top, peak[..., None])
        expos = [jnp.exp(s - new_top) for s in scores]
        part_denom = sum(jnp.sum(e, axis=-1, keepdims=True) for e in expos)
        part_mixed = sum(
            jnp.einsum(
                "fqk,fkc->fqc", e.astype(jnp.bfloat16), p, preferred_element_type=jnp.float32
            )
            for e, p in zip(expos, group)
        )
        if top is None:
            denom, mixed_in = part_denom, part_mixed
        else:
            shrink = jnp.exp(top - new_top)
            denom = denom * shrink + part_denom
            mixed_in = mixed_in * shrink + part_mixed
        top, denom, mixed_in = lax.optimization_barrier((new_top, denom, mixed_in))
    both = jnp.einsum(
        "fqc,cd->fqd", split_pair(mixed_in, axis=1), w_value, preferred_element_type=jnp.float32
    )
    numer = both[:, :count] + both[:, count:]
    attended = (numer / denom).astype(jnp.bfloat16)
    mixed = (
        flat.astype(jnp.float32)
        + jnp.einsum("fqc,cd->fqd", attended, w_out, preferred_element_type=jnp.float32)
    ).astype(jnp.bfloat16)
    activ = (
        jax.nn.silu(rms_gain(mixed.astype(jnp.float32), norm_conv))
        .astype(jnp.bfloat16)
        .reshape(nframes, nrows, ncols, chans)
    )
    centre = cache_part + tap_row(activ, conv_weight[2, 1])
    activ_haloed = padded_2(activ, ((ROWS, 1),), 1)
    edges = tap_row(activ_haloed[:, :nrows], conv_weight[2, 0]) + tap_row(
        activ_haloed[:, 2:], conv_weight[2, 2]
    )
    conv_out = (centre + edges).astype(jnp.bfloat16)
    extended = padded_2(conv_out, ((ROWS, 1),), 1)
    return upsample_conv(extended, w_up)


def solution(mesh):
    clips, rows = mesh.devices.shape
    mesh = jax.sharding.Mesh(mesh.devices.reshape(clips, rows // 2, 2), ("clips",) + ROWS)
    placed = (
        P("clips", ROWS, None, None),
        P(),
        P(),
        P(),
        P(),
        P(),
        P("clips", ROWS, None, None),
        P(),
        P(),
        P(),
    )
    return jax.shard_map(
        layer, mesh=mesh, in_specs=placed, out_specs=P("clips", ROWS, None), check_vma=False
    )
```

```python
import jax
import jax.numpy as jnp
from jax import lax
from jax.sharding import PartitionSpec as P


EPS = 1e-06


ROWS = ("chip", "core")


def padded_2(array, sides, width):
    for axis, dim in sides:
        size = lax.axis_size(axis)
        even = (lax.axis_index(axis) % 2) == 0
        first = lax.slice_in_dim(array, 0, width, axis=dim)
        last = lax.slice_in_dim(array, array.shape[dim] - width, array.shape[dim], axis=dim)
        pairs = [(i, i + 1) for i in range(1, size - 1, 2)]
        across = lax.ppermute(
            jnp.where(even, first, last), axis, pairs + [(j, i) for i, j in pairs]
        )
        on_chip = lax.ppermute(
            jnp.where(even, last, first), axis, [(i, i ^ 1) for i in range(size)]
        )
        before = jnp.where(even, across, on_chip)
        after = jnp.where(even, on_chip, across)
        array = jnp.concatenate([before, array, after], axis=dim)
    return array


def rms_gain(values, gain):
    return values * lax.rsqrt(jnp.mean(values * values, axis=-1, keepdims=True) + EPS) * gain


def project(inputs, weight):
    return jnp.einsum("fqc,cd->fqd", inputs, weight, preferred_element_type=jnp.float32).astype(
        jnp.bfloat16
    )


def exchange(values, bits, size):
    masks = [0]
    for bit in bits:
        masks = masks + [mask | bit for mask in masks]
    return [
        lax.ppermute(values, ROWS, [(i, i ^ mask) for i in range(size)]) for mask in masks[1:]
    ]


def tap_row(rows, weight):
    return lax.conv_general_dilated(
        rows,
        weight[None],
        window_strides=(1, 1),
        padding=((0, 0), (1, 1)),
        dimension_numbers=("NHWC", "HWIO", "NHWC"),
        preferred_element_type=jnp.float32,
    )


def split_pair(values, axis):
    high = values.astype(jnp.bfloat16)
    low = (values - high.astype(jnp.float32)).astype(jnp.bfloat16)
    return jnp.concatenate([high, low], axis=axis)


def conv_rows(haloed, weight):
    total = None
    for tstep in range(weight.shape[0]):
        part = lax.conv_general_dilated(
            haloed[tstep : tstep + 1],
            weight[tstep],
            window_strides=(1, 1),
            padding=((0, 0), (1, 1)),
            dimension_numbers=("NHWC", "HWIO", "NHWC"),
            preferred_element_type=jnp.float32,
        )
        total = part if total is None else total + part
    return total


def upsample_conv(extended, w_up):
    nf, rp, ncols, _ = extended.shape
    nrows = rp - 2
    outs = w_up.shape[-1]
    padded = jnp.pad(extended, ((0, 0), (0, 0), (1, 1), (0, 0)))
    taps = jnp.einsum(
        "frwc,ijco->frwijo", padded, w_up, preferred_element_type=jnp.float32
    )
    phases_a = []
    for a in range(2):
        phases_b = []
        for b in range(2):
            acc = None
            for dr in range(3):
                ro = (a + dr + 1) // 2
                for dc in range(3):
                    co = (b + dc + 1) // 2
                    term = taps[:, ro : ro + nrows, co : co + ncols, dr, dc, :]
                    acc = term if acc is None else acc + term
            phases_b.append(acc)
        phases_a.append(jnp.concatenate(phases_b, axis=-1))
    result = jnp.stack(phases_a, axis=2)
    return result.astype(jnp.bfloat16).reshape(nf, 2 * nrows, 2 * ncols * outs)


def layer(
    frames, norm_attn, w_query, w_key, w_value, w_out, cache_one, norm_conv, conv_weight, w_up
):
    nframes, nrows, ncols, chans = frames.shape
    scale = chans ** (-0.5)

    cache_haloed = padded_2(cache_one, ((ROWS, 1),), 1)
    cache_part = conv_rows(cache_haloed, conv_weight[:2])

    flat = frames.reshape(nframes, nrows * ncols, chans)
    normed = rms_gain(flat.astype(jnp.float32), norm_attn).astype(jnp.bfloat16)
    queries = project(normed, w_query)
    size = lax.axis_size(ROWS)
    chip_bits = [1 << k for k in range(1, size.bit_length() - 1)]
    low, high = chip_bits[:1], chip_bits[1:]
    half = normed.shape[1] // 2
    first, second = normed[:, :half], normed[:, half:]
    first_in = exchange(first, high, size)
    second_in = exchange(second, low, size)
    gathered = jnp.concatenate([first, second] + first_in + second_in, axis=1)
    first_out = exchange(jnp.concatenate([first] + first_in, axis=1), low, size)
    second_out = exchange(jnp.concatenate([second] + second_in, axis=1), high, size)
    mine = [gathered] + first_out + second_out
    mirrors = exchange(gathered, [1], size)
    mirrors = mirrors + [exchange(piece, [1], size)[0] for piece in mine[1:]]
    pieces = mine + mirrors
    q_keyed = jnp.einsum("fqc,dc->fqd", queries, w_key, preferred_element_type=jnp.float32)
    q_pair = split_pair(q_keyed, axis=1)
    count = queries.shape[1]
    groups = [[mine[0], pieces[len(mine)]], mine[1:], pieces[len(mine) + 1 :]]
    top = denom = mixed_in = None
    for number, group in enumerate(groups):
        scores = []
        for piece in group:
            if number + 1 < len(groups):
                both = jnp.einsum("fqc,fkc->fqk", q_pair, piece, preferred_element_type=jnp.float32)
                scores.append((both[:, :count] + both[:, count:]) * scale)
            else:
                scores.append(
                    jnp.einsum(
                        "fqc,fkc->fqk", q_pair[:, :count], piece,
                        preferred_element_type=jnp.float32,
                    )
                    * scale
                )
        peak = jnp.max(jnp.stack([jnp.max(s, axis=-1) for s in scores], axis=-1), axis=-1)
        new_top = peak[..., None] if top is None else jnp.maximum(top, peak[..., None])
        expos = [jnp.exp(s - new_top) for s in scores]
        part_denom = sum(jnp.sum(e, axis=-1, keepdims=True) for e in expos)
        part_mixed = sum(
            jnp.einsum(
                "fqk,fkc->fqc", e.astype(jnp.bfloat16), p, preferred_element_type=jnp.float32
            )
            for e, p in zip(expos, group)
        )
        if top is None:
            denom, mixed_in = part_denom, part_mixed
        else:
            shrink = jnp.exp(top - new_top)
            denom = denom * shrink + part_denom
            mixed_in = mixed_in * shrink + part_mixed
        top, denom, mixed_in = lax.optimization_barrier((new_top, denom, mixed_in))
    both = jnp.einsum(
        "fqc,cd->fqd", split_pair(mixed_in, axis=1), w_value, preferred_element_type=jnp.float32
    )
    numer = both[:, :count] + both[:, count:]
    attended = (numer / denom).astype(jnp.bfloat16)
    mixed = (
        flat.astype(jnp.float32)
        + jnp.einsum("fqc,cd->fqd", attended, w_out, preferred_element_type=jnp.float32)
    ).astype(jnp.bfloat16)
    activ = (
        jax.nn.silu(rms_gain(mixed.astype(jnp.float32), norm_conv))
        .astype(jnp.bfloat16)
        .reshape(nframes, nrows, ncols, chans)
    )
    centre = cache_part + tap_row(activ, conv_weight[2, 1])
    activ_haloed = padded_2(activ, ((ROWS, 1),), 1)
    edges = tap_row(activ_haloed[:, :nrows], conv_weight[2, 0]) + tap_row(
        activ_haloed[:, 2:], conv_weight[2, 2]
    )
    conv_out = (centre + edges).astype(jnp.bfloat16)
    extended = padded_2(conv_out, ((ROWS, 1),), 1)
    return upsample_conv(extended, w_up)


def solution(mesh):
    clips, rows = mesh.devices.shape
    mesh = jax.sharding.Mesh(mesh.devices.reshape(clips, rows // 2, 2), ("clips",) + ROWS)
    placed = (
        P("clips", ROWS, None, None),
        P(),
        P(),
        P(),
        P(),
        P(),
        P("clips", ROWS, None, None),
        P(),
        P(),
        P(),
    )
    return jax.shard_map(
        layer, mesh=mesh, in_specs=placed, out_specs=P("clips", ROWS, None), check_vma=False
    )
```

```python
import jax
import jax.numpy as jnp
from jax import lax
from jax.sharding import PartitionSpec as P


EPS = 1e-06


ROWS = ("chip", "core")


def padded_2(array, sides, width):
    for axis, dim in sides:
        size = lax.axis_size(axis)
        even = (lax.axis_index(axis) % 2) == 0
        first = lax.slice_in_dim(array, 0, width, axis=dim)
        last = lax.slice_in_dim(array, array.shape[dim] - width, array.shape[dim], axis=dim)
        pairs = [(i, i + 1) for i in range(1, size - 1, 2)]
        across = lax.ppermute(
            jnp.where(even, first, last), axis, pairs + [(j, i) for i, j in pairs]
        )
        on_chip = lax.ppermute(
            jnp.where(even, last, first), axis, [(i, i ^ 1) for i in range(size)]
        )
        before = jnp.where(even, across, on_chip)
        after = jnp.where(even, on_chip, across)
        array = jnp.concatenate([before, array, after], axis=dim)
    return array


def rms_gain(values, gain):
    return values * lax.rsqrt(jnp.mean(values * values, axis=-1, keepdims=True) + EPS) * gain


def project(inputs, weight):
    return jnp.einsum("fqc,cd->fqd", inputs, weight, preferred_element_type=jnp.float32).astype(
        jnp.bfloat16
    )


def exchange(values, bits, size):
    masks = [0]
    for bit in bits:
        masks = masks + [mask | bit for mask in masks]
    return [
        lax.ppermute(values, ROWS, [(i, i ^ mask) for i in range(size)]) for mask in masks[1:]
    ]


def tap_row(rows, weight):
    return lax.conv_general_dilated(
        rows,
        weight[None],
        window_strides=(1, 1),
        padding=((0, 0), (1, 1)),
        dimension_numbers=("NHWC", "HWIO", "NHWC"),
        preferred_element_type=jnp.float32,
    )


def split_pair(values, axis):
    high = values.astype(jnp.bfloat16)
    low = (values - high.astype(jnp.float32)).astype(jnp.bfloat16)
    return jnp.concatenate([high, low], axis=axis)


def conv_rows(haloed, weight):
    total = None
    for tstep in range(weight.shape[0]):
        part = lax.conv_general_dilated(
            haloed[tstep : tstep + 1],
            weight[tstep],
            window_strides=(1, 1),
            padding=((0, 0), (1, 1)),
            dimension_numbers=("NHWC", "HWIO", "NHWC"),
            preferred_element_type=jnp.float32,
        )
        total = part if total is None else total + part
    return total


def upsample_conv(extended, w_up):
    nf, rp, ncols, _ = extended.shape
    nrows = rp - 2
    outs = w_up.shape[-1]
    padded = jnp.pad(extended, ((0, 0), (0, 0), (1, 1), (0, 0)))
    taps = jnp.einsum(
        "frwc,ijco->frwijo", padded, w_up, preferred_element_type=jnp.float32
    )
    phases_a = []
    for a in range(2):
        phases_b = []
        for b in range(2):
            acc = None
            for dr in range(3):
                ro = (a + dr + 1) // 2
                for dc in range(3):
                    co = (b + dc + 1) // 2
                    term = taps[:, ro : ro + nrows, co : co + ncols, dr, dc, :]
                    acc = term if acc is None else acc + term
            phases_b.append(acc)
        phases_a.append(jnp.concatenate(phases_b, axis=-1))
    result = jnp.stack(phases_a, axis=2)
    return result.astype(jnp.bfloat16).reshape(nf, 2 * nrows, 2 * ncols * outs)


def layer(
    frames, norm_attn, w_query, w_key, w_value, w_out, cache_one, norm_conv, conv_weight, w_up
):
    nframes, nrows, ncols, chans = frames.shape
    scale = chans ** (-0.5)

    cache_haloed = padded_2(cache_one, ((ROWS, 1),), 1)
    cache_part = conv_rows(cache_haloed, conv_weight[:2])

    flat = frames.reshape(nframes, nrows * ncols, chans)
    normed = rms_gain(flat.astype(jnp.float32), norm_attn).astype(jnp.bfloat16)
    queries = project(normed, w_query)
    size = lax.axis_size(ROWS)
    chip_bits = [1 << k for k in range(1, size.bit_length() - 1)]
    low, high = chip_bits[:1], chip_bits[1:]
    half = normed.shape[1] // 2
    first, second = normed[:, :half], normed[:, half:]
    first_in = exchange(first, high, size)
    second_in = exchange(second, low, size)
    gathered = jnp.concatenate([first, second] + first_in + second_in, axis=1)
    first_out = exchange(jnp.concatenate([first] + first_in, axis=1), low, size)
    second_out = exchange(jnp.concatenate([second] + second_in, axis=1), high, size)
    mine = [gathered] + first_out + second_out
    mirrors = exchange(gathered, [1], size)
    mirrors = mirrors + exchange(jnp.concatenate(mine[1:], axis=1), [1], size)
    pieces = mine + mirrors
    q_keyed = jnp.einsum("fqc,dc->fqd", queries, w_key, preferred_element_type=jnp.float32)
    q_pair = split_pair(q_keyed, axis=1)
    count = queries.shape[1]
    groups = [[mine[0], pieces[len(mine)]], mine[1:], pieces[len(mine) + 1 :]]
    top = denom = mixed_in = None
    for group in groups:
        scores = []
        for piece in group:
            both = jnp.einsum("fqc,fkc->fqk", q_pair, piece, preferred_element_type=jnp.float32)
            scores.append((both[:, :count] + both[:, count:]) * scale)
        peak = jnp.max(jnp.stack([jnp.max(s, axis=-1) for s in scores], axis=-1), axis=-1)
        new_top = peak[..., None] if top is None else jnp.maximum(top, peak[..., None])
        expos = [jnp.exp(s - new_top) for s in scores]
        part_denom = sum(jnp.sum(e, axis=-1, keepdims=True) for e in expos)
        part_mixed = sum(
            jnp.einsum(
                "fqk,fkc->fqc", e.astype(jnp.bfloat16), p, preferred_element_type=jnp.float32
            )
            for e, p in zip(expos, group)
        )
        if top is None:
            denom, mixed_in = part_denom, part_mixed
        else:
            shrink = jnp.exp(top - new_top)
            denom = denom * shrink + part_denom
            mixed_in = mixed_in * shrink + part_mixed
        top, denom, mixed_in = lax.optimization_barrier((new_top, denom, mixed_in))
    both = jnp.einsum(
        "fqc,cd->fqd", split_pair(mixed_in, axis=1), w_value, preferred_element_type=jnp.float32
    )
    numer = both[:, :count] + both[:, count:]
    attended = (numer / denom).astype(jnp.bfloat16)
    mixed = (
        flat.astype(jnp.float32)
        + jnp.einsum("fqc,cd->fqd", attended, w_out, preferred_element_type=jnp.float32)
    ).astype(jnp.bfloat16)
    activ = (
        jax.nn.silu(rms_gain(mixed.astype(jnp.float32), norm_conv))
        .astype(jnp.bfloat16)
        .reshape(nframes, nrows, ncols, chans)
    )
    centre = cache_part + tap_row(activ, conv_weight[2, 1])
    activ_haloed = padded_2(activ, ((ROWS, 1),), 1)
    edges = tap_row(activ_haloed[:, :nrows], conv_weight[2, 0]) + tap_row(
        activ_haloed[:, 2:], conv_weight[2, 2]
    )
    conv_out = (centre + edges).astype(jnp.bfloat16)
    extended = padded_2(conv_out, ((ROWS, 1),), 1)
    return upsample_conv(extended, w_up)


def solution(mesh):
    clips, rows = mesh.devices.shape
    mesh = jax.sharding.Mesh(mesh.devices.reshape(clips, rows // 2, 2), ("clips",) + ROWS)
    placed = (
        P("clips", ROWS, None, None),
        P(),
        P(),
        P(),
        P(),
        P(),
        P("clips", ROWS, None, None),
        P(),
        P(),
        P(),
    )
    return jax.shard_map(
        layer, mesh=mesh, in_specs=placed, out_specs=P("clips", ROWS, None), check_vma=False
    )
```
